128 devices in a mesh: blk: 32 (over z, y, x_hi), grp: 4 (over x_lo, core).
Axes of the slice: x: 4 (x_hi: 2, x_lo: 2; x = x_hi * 2 + x_lo), y: 4, z: 4, core: 2. Of those that a mesh axis runs over, the one named last changes fastest.
Arguments:
- queries: bfloat16 [65536, 2048], P('blk', 'grp'), may hold values from -64 to 64
- encoder: bfloat16 [4096, 2048], P('blk'), may hold values from -6 to 6
- key_weight: bfloat16 [2048, 2048], P(None, 'grp'), may hold values from -0.125 to 0.125
- value_weight: bfloat16 [2048, 2048], P(None, 'grp'), may hold values from -0.125 to 0.125
- out_grad: bfloat16 [65536, 2048], P('blk', 'grp'), may hold values from -6 to 6
- block_lists: int32 [512, 5], P('blk'), may hold values from 0 to 31, as said below
- list_counts: int32 [512], P('blk'), may hold values from 1 to 5, as said below
Outputs:
- attended: bfloat16 [65536, 2048], P('blk', 'grp')
- query_grad: bfloat16 [65536, 2048], P('blk', 'grp')
- encoder_grad: bfloat16 [4096, 2048], P('blk', 'grp')
- key_weight_grad: float32 [2048, 2048], P('blk', 'grp')
- value_weight_grad: float32 [2048, 2048], P('blk', 'grp')
The draws below stay inside these ranges and needn't reach their ends.
Inputs may be any that keep to these rules, and one draw needn't show every extreme that they name: `block_lists`: query block b belongs to blk index b // 16. Each list holds 5 distinct encoder block ids, all within 4 of that index; every blk index has a query block whose list reaches exactly 4 blocks away, and entries past list_counts are valid but unused ids. `list_counts`: every blk index has a query block that uses all 5 entries.
All inputs are finite; a program needn't handle non-finite values.
Results may differ from the reference program's by a relative error of at most 0.015.
The reference program's roundings to bfloat16 on the way (of `key_rows`, `value_rows`, `weights`, `dscores`, `key_grad` and `value_grad`) count: a program that leaves them out, or rounds other values in their place, can miss the bound.
Values may be sent and summed in bfloat16 or wider, within the bound.
No kernel may reach another device: no remote copies, remote signals or barrier semaphores. Data moves between devices by JAX's collectives and lax.ppermute only.
A program may use at most 128 MiB of HBM per device.

```python
import jax
import jax.numpy as jnp
from jax import lax

D = 2048
HEADS = 32
HEAD_DIM = 64
BLOCK = 128
REACH = 4
LISTED = 5
QB_DEV = 16
INNER = 2048
QBLOCKS = 512
QROWS = 65536
EBLOCKS = 32
ENC = 4096


def draw_queries(key, part):
    normal_key = jax.random.fold_in(jax.random.fold_in(key, 11), 0)
    return jnp.clip(jax.random.normal(normal_key, (QROWS, INNER), jnp.float32), -6.0, 6.0).astype(jnp.bfloat16)


def lists_and_counts(key):
    order_key, count_key = jax.random.split(jax.random.fold_in(key, 29))
    width_all = 2 * REACH + 1
    qblock = jnp.arange(QBLOCKS, dtype=jnp.int32)
    owner = qblock // QB_DEV
    local = qblock % QB_DEV
    offsets = jnp.arange(width_all, dtype=jnp.int32) - REACH
    block_ids = owner[:, None] + offsets[None, :]
    inside = (block_ids >= 0) & (block_ids < EBLOCKS)
    ranking = jax.random.randint(order_key, (QBLOCKS, width_all), 0, 1000) * 64 + jnp.arange(width_all, dtype=jnp.int32)[None, :]
    ranking = jnp.where(inside, ranking, ranking + 10000000)
    first_far = jnp.where(owner >= REACH, -REACH, REACH)
    second_far = jnp.where(owner + REACH < EBLOCKS, REACH, -REACH)
    forced = jnp.where(local == 0, first_far, jnp.where(local == 1, second_far, 1000))
    ranking = jnp.where(offsets[None, :] == forced[:, None], -1, ranking)
    order = jnp.argsort(ranking, axis=1)
    chosen = jnp.take_along_axis(block_ids, order, axis=1)[:, :LISTED].astype(jnp.int32)
    counts = jax.random.randint(count_key, (QBLOCKS,), 1, LISTED + 1)
    counts = jnp.where(local == 0, LISTED, counts).astype(jnp.int32)
    return (chosen, counts)


def draw_block_lists(key, part):
    return lists_and_counts(key)[0]


def draw_list_counts(key, part):
    return lists_and_counts(key)[1]


def spiked(array, stream_key, source, target, blocks, factor):
    owner, partner = [(jnp.arange(array.shape[position]) // (array.shape[position] // blocks)).reshape([-1 if axis == position else 1 for axis in range(array.ndim)]) for position in (source, target)]
    chosen = jax.random.permutation(stream_key, blocks)[partner]
    strong = (owner == chosen) | (owner == (partner + blocks // 2) % blocks)
    return jnp.where(strong, factor * array, array)


def shard_levels(key, dims, cuts, smallest, top_value):
    factor_of, own = 1.0, jax.random.fold_in(key, 6)
    for position, shards_of in cuts:
        heights = jnp.exp(jax.random.uniform(jax.random.fold_in(own, position), (shards_of,), jnp.float32, smallest / len(cuts), top_value / len(cuts)))
        factor_of = factor_of * jnp.repeat(heights, dims[position] // shards_of).reshape([-1 if axis == position else 1 for axis in range(len(dims))])
    return factor_of


def noise(key, shape, width, reach, cuts=(), kind=jnp.bfloat16):
    array = jax.random.normal(key, shape, jnp.float32) * width
    if len(cuts) > 0:
        array = shard_levels(key, shape, cuts, -0.22, 0.18) * array
    return jnp.clip(array, min=-reach, max=reach).astype(kind)


def noise_with(key, shape, deviation, reach, cuts, heavy, kind=jnp.bfloat16):
    values = deviation * jax.random.normal(key, shape, jnp.float32)
    if cuts:
        values = values * shard_levels(key, shape, cuts, -0.22, 0.18)
    return jnp.clip(spiked(values, jax.random.fold_in(key, 3), *heavy), -reach, reach).astype(kind)


def setup_inputs(seed: int = 0) -> dict:
    streams_of = jax.random.split(jax.random.key(seed), 8)
    queries = draw_queries(jax.random.fold_in(streams_of[7], 71), 0)
    encoder = noise_with(streams_of[1], (ENC, D), 1.0, 6.0, ((0, 32),), (0, 1, 32, 2.75))
    key_weight = noise(streams_of[2], (D, INNER), D ** -0.5, 0.125, ((1, 4),))
    value_weight = noise(streams_of[3], (D, INNER), D ** -0.5, 0.125, ((1, 4),))
    out_grad = noise(streams_of[4], (QROWS, INNER), 1.0, 6.0, ((0, 32), (1, 4)))
    block_lists = draw_block_lists(jax.random.fold_in(streams_of[7], 71), 0)
    list_counts = draw_list_counts(jax.random.fold_in(streams_of[7], 71), 0)
    return dict(queries=queries, encoder=encoder, key_weight=key_weight, value_weight=value_weight, out_grad=out_grad, block_lists=block_lists, list_counts=list_counts)


def reference(queries, encoder, key_weight, value_weight, out_grad, block_lists, list_counts):
    factor = HEAD_DIM ** -0.5
    key_rows = jnp.dot(encoder, key_weight, preferred_element_type=jnp.float32).astype(jnp.bfloat16)
    value_rows = jnp.dot(encoder, value_weight, preferred_element_type=jnp.float32).astype(jnp.bfloat16)
    key_blocks = key_rows.reshape(EBLOCKS, BLOCK, HEADS, HEAD_DIM)
    value_blocks = value_rows.reshape(EBLOCKS, BLOCK, HEADS, HEAD_DIM)
    query_blocks = queries.reshape(QBLOCKS, BLOCK, HEADS, HEAD_DIM)
    grad_blocks = out_grad.reshape(QBLOCKS, BLOCK, HEADS, HEAD_DIM)

    def visit(carry, item):
        key_sum, value_sum = carry
        query, grad, listed, count = item
        usable = jnp.arange(LISTED, dtype=jnp.int32) < count
        keep_keys = jnp.repeat(usable, BLOCK)
        picked_keys = key_blocks[listed].reshape(LISTED * BLOCK, HEADS, HEAD_DIM).astype(jnp.float32)
        picked_values = value_blocks[listed].reshape(LISTED * BLOCK, HEADS, HEAD_DIM).astype(jnp.float32)
        query_full = query.astype(jnp.float32)
        grad_full = grad.astype(jnp.float32)
        scores = jnp.einsum("qhd,khd->hqk", query_full, picked_keys) * factor
        scores = jnp.where(keep_keys[None, None, :], scores, -jnp.inf)
        peak = jnp.max(scores, axis=-1, keepdims=True)
        expo = jnp.exp(scores - peak)
        weights_low = (expo / jnp.sum(expo, axis=-1, keepdims=True)).astype(jnp.bfloat16)
        weights = lax.optimization_barrier(weights_low).astype(jnp.float32)
        output = jnp.einsum("hqk,khd->qhd", weights, picked_values).astype(jnp.bfloat16)
        dweights = jnp.einsum("qhd,khd->hqk", grad_full, picked_values)
        center = jnp.sum(weights * dweights, axis=-1, keepdims=True)
        dscores_low = (weights * (dweights - center) * factor).astype(jnp.bfloat16)
        dscores = lax.optimization_barrier(dscores_low).astype(jnp.float32)
        dquery = jnp.einsum("hqk,khd->qhd", dscores, picked_keys).astype(jnp.bfloat16)
        dkey = jnp.einsum("hqk,qhd->khd", dscores, query_full).reshape(LISTED, BLOCK, HEADS, HEAD_DIM)
        dvalue = jnp.einsum("hqk,qhd->khd", weights, grad_full).reshape(LISTED, BLOCK, HEADS, HEAD_DIM)
        key_sum = key_sum.at[listed].add(dkey)
        value_sum = value_sum.at[listed].add(dvalue)
        return (key_sum, value_sum), (output, dquery)

    start_sums = (jnp.zeros((EBLOCKS, BLOCK, HEADS, HEAD_DIM), jnp.float32),
                  jnp.zeros((EBLOCKS, BLOCK, HEADS, HEAD_DIM), jnp.float32))
    (key_sum, value_sum), (outputs, dqueries) = lax.scan(
        visit, start_sums, (query_blocks, grad_blocks, block_lists, list_counts))
    attended = outputs.reshape(QROWS, INNER)
    query_grad = dqueries.reshape(QROWS, INNER)
    key_grad = key_sum.reshape(ENC, INNER).astype(jnp.bfloat16)
    value_grad = value_sum.reshape(ENC, INNER).astype(jnp.bfloat16)
    encoder_full = (jnp.dot(key_grad, key_weight.T, preferred_element_type=jnp.float32)
                    + jnp.dot(value_grad, value_weight.T, preferred_element_type=jnp.float32))
    encoder_grad = encoder_full.astype(jnp.bfloat16)
    key_weight_grad = jnp.dot(encoder.T, key_grad, preferred_element_type=jnp.float32)
    value_weight_grad = jnp.dot(encoder.T, value_grad, preferred_element_type=jnp.float32)
    return attended, query_grad, encoder_grad, key_weight_grad, value_weight_grad
```

```python
import functools

import jax
import jax.numpy as jnp
from jax import lax
from jax.experimental import pallas as pl
from jax.experimental.pallas import tpu as pltpu
from jax.sharding import PartitionSpec as P

HEAD_DIM = 64
REACH = 4
LISTED = 5
LANES = 128


def passed_along(value, axis, by):
    size = lax.axis_size(axis)
    pairs = [(i, i + by) for i in range(size) if 0 <= i + by < size]
    return lax.ppermute(value, axis, pairs)


def attention_kernel(slots_ref, counts_ref, q_ref, g_ref, stock_ref, out_ref, dq_ref, acc_ref):
    factor = HEAD_DIM ** (-0.5)
    step = pl.program_id(0)

    @pl.when(step == 0)
    def _():
        acc_ref[...] = jnp.zeros_like(acc_ref)

    count = counts_ref[step]
    rows = q_ref.shape[0]
    lane = lax.broadcasted_iota(jnp.int32, (rows, LANES), 1)
    first = lane < HEAD_DIM
    slots = [slots_ref[step, j] for j in range(LISTED)]
    nt = (((1,), (1,)), ((), ()))
    tn = (((0,), (0,)), ((), ()))
    f32 = jnp.float32
    bf16 = jnp.bfloat16

    def pair(p, carry):
        off = pl.multiple_of(p * LANES, LANES)
        qp = q_ref[:, pl.ds(off, LANES)]
        gp = g_ref[:, pl.ds(off, LANES)]
        zq = jnp.zeros_like(qp)
        qh = [jnp.where(first, qp, zq), jnp.where(first, zq, qp)]
        gh = [jnp.where(first, gp, zq), jnp.where(first, zq, gp)]
        ks = [stock_ref[slots[j], 0, :, pl.ds(off, LANES)] for j in range(LISTED)]
        vs = [stock_ref[slots[j], 1, :, pl.ds(off, LANES)] for j in range(LISTED)]
        outs, dqs = [], []
        dks = [None] * LISTED
        dvs = [None] * LISTED
        for h in range(2):
            scores = []
            for j in range(LISTED):
                sc = lax.dot_general(qh[h], ks[j], nt, preferred_element_type=f32) * factor
                scores.append(jnp.where(j < count, sc, -jnp.inf))
            peak = jnp.max(scores[0], axis=1, keepdims=True)
            for j in range(1, LISTED):
                peak = jnp.maximum(peak, jnp.max(scores[j], axis=1, keepdims=True))
            expos = [jnp.exp(sc - peak) for sc in scores]
            total = jnp.sum(expos[0], axis=1, keepdims=True)
            for j in range(1, LISTED):
                total = total + jnp.sum(expos[j], axis=1, keepdims=True)
            ws = [(e / total).astype(bf16) for e in expos]
            out = jnp.dot(ws[0], vs[0], preferred_element_type=f32)
            for j in range(1, LISTED):
                out = out + jnp.dot(ws[j], vs[j], preferred_element_type=f32)
            dws = [lax.dot_general(gh[h], vs[j], nt, preferred_element_type=f32) for j in range(LISTED)]
            wf = [w.astype(f32) for w in ws]
            center = jnp.sum(wf[0] * dws[0], axis=1, keepdims=True)
            for j in range(1, LISTED):
                center = center + jnp.sum(wf[j] * dws[j], axis=1, keepdims=True)
            dss = [(wf[j] * (dws[j] - center) * factor).astype(bf16) for j in range(LISTED)]
            dq = jnp.dot(dss[0], ks[0], preferred_element_type=f32)
            for j in range(1, LISTED):
                dq = dq + jnp.dot(dss[j], ks[j], preferred_element_type=f32)
            for j in range(LISTED):
                dk = lax.dot_general(dss[j], qh[h], tn, preferred_element_type=f32)
                dv = lax.dot_general(ws[j], gh[h], tn, preferred_element_type=f32)
                dks[j] = dk if dks[j] is None else dks[j] + dk
                dvs[j] = dv if dvs[j] is None else dvs[j] + dv
            outs.append(out)
            dqs.append(dq)
        out_ref[:, pl.ds(off, LANES)] = jnp.where(first, outs[0], outs[1]).astype(out_ref.dtype)
        dq_ref[:, pl.ds(off, LANES)] = jnp.where(first, dqs[0], dqs[1]).astype(dq_ref.dtype)
        for j in range(LISTED):
            acc_ref[slots[j], 0, :, pl.ds(off, LANES)] += dks[j]
            acc_ref[slots[j], 1, :, pl.ds(off, LANES)] += dvs[j]
        return carry

    lax.fori_loop(0, q_ref.shape[1] // LANES, pair, 0)


def attention(queries, out_grad, stock, slot_ids, counts):
    rows, cols = stock.shape[2], stock.shape[3]
    blocks = queries.shape[0] // rows
    n_slots = stock.shape[0]
    flops = blocks * (cols // LANES) * 2 * LISTED * 6 * 2 * rows * LANES * LANES
    bytes_accessed = 4 * queries.size * 2 + stock.size * 2 + stock.size * 4
    grid_spec = pltpu.PrefetchScalarGridSpec(
        num_scalar_prefetch=2,
        grid=(blocks,),
        in_specs=[
            pl.BlockSpec((rows, cols), lambda i, s, c: (i, 0)),
            pl.BlockSpec((rows, cols), lambda i, s, c: (i, 0)),
            pl.BlockSpec((n_slots, 2, rows, cols), lambda i, s, c: (0, 0, 0, 0)),
        ],
        out_specs=[
            pl.BlockSpec((rows, cols), lambda i, s, c: (i, 0)),
            pl.BlockSpec((rows, cols), lambda i, s, c: (i, 0)),
            pl.BlockSpec((n_slots, 2, rows, cols), lambda i, s, c: (0, 0, 0, 0)),
        ],
    )
    return pl.pallas_call(
        attention_kernel,
        grid_spec=grid_spec,
        out_shape=[
            jax.ShapeDtypeStruct(queries.shape, jnp.bfloat16),
            jax.ShapeDtypeStruct(queries.shape, jnp.bfloat16),
            jax.ShapeDtypeStruct(stock.shape, jnp.float32),
        ],
        compiler_params=pltpu.CompilerParams(dimension_semantics=("arbitrary",)),
        cost_estimate=pl.CostEstimate(
            flops=flops, transcendentals=blocks * rows * LISTED * rows * (cols // HEAD_DIM),
            bytes_accessed=bytes_accessed,
        ),
    )(slot_ids, counts, queries, out_grad, stock)


def on_device(queries, encoder, key_weight, value_weight, out_grad, block_lists, list_counts):
    position = lax.axis_index("blk")
    head_cols = key_weight.shape[1]
    own_keys = jnp.dot(encoder, key_weight, preferred_element_type=jnp.float32).astype(jnp.bfloat16)
    own_values = jnp.dot(encoder, value_weight, preferred_element_type=jnp.float32).astype(
        jnp.bfloat16
    )
    own = jnp.stack([own_keys, own_values], 0)
    arrived = []
    for offset in range(-REACH, REACH + 1):
        if offset == 0:
            arrived.append(own)
        else:
            arrived.append(passed_along(own, "blk", -offset))
    stock = jnp.stack(arrived, 0)
    slot_ids = (block_lists - (position - REACH)).astype(jnp.int32)
    attended, query_grad, running = attention(
        queries, out_grad, stock, slot_ids, list_counts.astype(jnp.int32)
    )
    owned = running[REACH]
    for offset in range(-REACH, REACH + 1):
        if offset != 0:
            owned = owned + passed_along(running[REACH + offset], "blk", offset)
    rounded = owned.astype(jnp.bfloat16)
    contract_cols = (((1,), (1,)), ((), ()))
    encoder_terms = lax.dot_general(
        rounded[0], key_weight, contract_cols, preferred_element_type=jnp.float32
    ) + lax.dot_general(rounded[1], value_weight, contract_cols, preferred_element_type=jnp.float32)
    encoder_grad = lax.psum_scatter(encoder_terms, "grp", scatter_dimension=1, tiled=True).astype(
        jnp.bfloat16
    )
    both_grads = jnp.concatenate([rounded[0], rounded[1]], 1)
    weight_rows = lax.psum_scatter(
        lax.dot_general(
            encoder, both_grads, (((0,), (0,)), ((), ())), preferred_element_type=jnp.float32
        ),
        "blk",
        scatter_dimension=0,
        tiled=True,
    )
    return (
        attended,
        query_grad,
        encoder_grad,
        weight_rows[:, :head_cols],
        weight_rows[:, head_cols:],
    )


def solution(mesh):
    in_specs = (
        P("blk", "grp"),
        P("blk", None),
        P(None, "grp"),
        P(None, "grp"),
        P("blk", "grp"),
        P("blk", None),
        P("blk"),
    )
    out_specs = (
        P("blk", "grp"),
        P("blk", "grp"),
        P("blk", "grp"),
        P("blk", "grp"),
        P("blk", "grp"),
    )
    return jax.shard_map(
        on_device, mesh=mesh, in_specs=in_specs, out_specs=out_specs, check_vma=False
    )
```

```python
import functools

import jax
import jax.numpy as jnp
from jax import lax
from jax.experimental import pallas as pl
from jax.experimental.pallas import tpu as pltpu
from jax.sharding import PartitionSpec as P

HEAD_DIM = 64
REACH = 4
LISTED = 5
LANES = 128


def passed_along(value, axis, by, size):
    pairs = [(i, i + by) for i in range(size) if 0 <= i + by < size]
    return lax.ppermute(value, axis, pairs)


def attention_kernel(slots_ref, counts_ref, q_ref, g_ref, stock_ref, out_ref, dq_ref, acc_ref):
    factor = HEAD_DIM ** (-0.5)
    step = pl.program_id(0)

    @pl.when(step == 0)
    def _():
        acc_ref[...] = jnp.zeros_like(acc_ref)

    count = counts_ref[step]
    rows = q_ref.shape[0]
    lane = lax.broadcasted_iota(jnp.int32, (rows, LANES), 1)
    first = lane < HEAD_DIM
    slots = [slots_ref[step, j] for j in range(LISTED)]
    nt = (((1,), (1,)), ((), ()))
    tn = (((0,), (0,)), ((), ()))
    f32 = jnp.float32
    bf16 = jnp.bfloat16

    def pair(p, carry):
        off = pl.multiple_of(p * LANES, LANES)
        qp = q_ref[:, pl.ds(off, LANES)]
        gp = g_ref[:, pl.ds(off, LANES)]
        zq = jnp.zeros_like(qp)
        qh = [jnp.where(first, qp, zq), jnp.where(first, zq, qp)]
        gh = [jnp.where(first, gp, zq), jnp.where(first, zq, gp)]
        ks = [stock_ref[slots[j], 0, :, pl.ds(off, LANES)] for j in range(LISTED)]
        vs = [stock_ref[slots[j], 1, :, pl.ds(off, LANES)] for j in range(LISTED)]
        outs, dqs = [], []
        dks = [None] * LISTED
        dvs = [None] * LISTED
        for h in range(2):
            scores = []
            for j in range(LISTED):
                sc = lax.dot_general(qh[h], ks[j], nt, preferred_element_type=f32) * factor
                scores.append(jnp.where(j < count, sc, -jnp.inf))
            peak = jnp.max(scores[0], axis=1, keepdims=True)
            for j in range(1, LISTED):
                peak = jnp.maximum(peak, jnp.max(scores[j], axis=1, keepdims=True))
            expos = [jnp.exp(sc - peak) for sc in scores]
            total = jnp.sum(expos[0], axis=1, keepdims=True)
            for j in range(1, LISTED):
                total = total + jnp.sum(expos[j], axis=1, keepdims=True)
            ws = [(e / total).astype(bf16) for e in expos]
            out = jnp.dot(ws[0], vs[0], preferred_element_type=f32)
            for j in range(1, LISTED):
                out = out + jnp.dot(ws[j], vs[j], preferred_element_type=f32)
            dws = [lax.dot_general(gh[h], vs[j], nt, preferred_element_type=f32) for j in range(LISTED)]
            wf = [w.astype(f32) for w in ws]
            center = jnp.sum(wf[0] * dws[0], axis=1, keepdims=True)
            for j in range(1, LISTED):
                center = center + jnp.sum(wf[j] * dws[j], axis=1, keepdims=True)
            dss = [(wf[j] * (dws[j] - center) * factor).astype(bf16) for j in range(LISTED)]
            dq = jnp.dot(dss[0], ks[0], preferred_element_type=f32)
            for j in range(1, LISTED):
                dq = dq + jnp.dot(dss[j], ks[j], preferred_element_type=f32)
            for j in range(LISTED):
                dk = lax.dot_general(dss[j], qh[h], tn, preferred_element_type=f32)
                dv = lax.dot_general(ws[j], gh[h], tn, preferred_element_type=f32)
                dks[j] = dk if dks[j] is None else dks[j] + dk
                dvs[j] = dv if dvs[j] is None else dvs[j] + dv
            outs.append(out)
            dqs.append(dq)
        out_ref[:, pl.ds(off, LANES)] = jnp.where(first, outs[0], outs[1]).astype(out_ref.dtype)
        dq_ref[:, pl.ds(off, LANES)] = jnp.where(first, dqs[0], dqs[1]).astype(dq_ref.dtype)
        for j in range(LISTED):
            acc_ref[slots[j], 0, :, pl.ds(off, LANES)] += dks[j]
            acc_ref[slots[j], 1, :, pl.ds(off, LANES)] += dvs[j]
        return carry

    lax.fori_loop(0, q_ref.shape[1] // LANES, pair, 0)


def attention(queries, out_grad, stock, slot_ids, counts):
    rows, cols = stock.shape[2], stock.shape[3]
    blocks = queries.shape[0] // rows
    n_slots = stock.shape[0]
    flops = blocks * (cols // LANES) * 2 * LISTED * 6 * 2 * rows * LANES * LANES
    bytes_accessed = 4 * queries.size * 2 + stock.size * 2 + stock.size * 4
    grid_spec = pltpu.PrefetchScalarGridSpec(
        num_scalar_prefetch=2,
        grid=(blocks,),
        in_specs=[
            pl.BlockSpec((rows, cols), lambda i, s, c: (i, 0)),
            pl.BlockSpec((rows, cols), lambda i, s, c: (i, 0)),
            pl.BlockSpec((n_slots, 2, rows, cols), lambda i, s, c: (0, 0, 0, 0)),
        ],
        out_specs=[
            pl.BlockSpec((rows, cols), lambda i, s, c: (i, 0)),
            pl.BlockSpec((rows, cols), lambda i, s, c: (i, 0)),
            pl.BlockSpec((n_slots, 2, rows, cols), lambda i, s, c: (0, 0, 0, 0)),
        ],
    )
    return pl.pallas_call(
        attention_kernel,
        grid_spec=grid_spec,
        out_shape=[
            jax.ShapeDtypeStruct(queries.shape, jnp.bfloat16),
            jax.ShapeDtypeStruct(queries.shape, jnp.bfloat16),
            jax.ShapeDtypeStruct(stock.shape, jnp.float32),
        ],
        compiler_params=pltpu.CompilerParams(dimension_semantics=("arbitrary",)),
        cost_estimate=pl.CostEstimate(
            flops=flops, transcendentals=blocks * rows * LISTED * rows * (cols // HEAD_DIM),
            bytes_accessed=bytes_accessed,
        ),
    )(slot_ids, counts, queries, out_grad, stock)


def on_device(
    queries, encoder, key_weight, value_weight, out_grad, block_lists, list_counts, outer, inner
):
    blk = ("bz", "byx")
    position = lax.axis_index(blk)
    head_cols = key_weight.shape[1]
    model = encoder.shape[1]
    near = lax.all_gather(encoder, "byx", axis=0, tiled=False)
    own_keys = jnp.dot(encoder, key_weight, preferred_element_type=jnp.float32).astype(jnp.bfloat16)
    own_values = jnp.dot(encoder, value_weight, preferred_element_type=jnp.float32).astype(
        jnp.bfloat16
    )
    own = jnp.stack([own_keys, own_values], 0)
    arrived = []
    for offset in range(-REACH, REACH + 1):
        if offset == 0:
            arrived.append(own)
        else:
            arrived.append(passed_along(own, blk, -offset, outer * inner))
    stock = jnp.stack(arrived, 0)
    slot_ids = (block_lists - (position - REACH)).astype(jnp.int32)
    attended, query_grad, running = attention(
        queries, out_grad, stock, slot_ids, list_counts.astype(jnp.int32)
    )
    owned = running[REACH]
    for offset in range(-REACH, REACH + 1):
        if offset != 0:
            owned = owned + passed_along(running[REACH + offset], blk, offset, outer * inner)
    rounded = owned.astype(jnp.bfloat16)
    contract_cols = (((1,), (1,)), ((), ()))
    encoder_terms = lax.dot_general(
        rounded[0], key_weight, contract_cols, preferred_element_type=jnp.float32
    ) + lax.dot_general(rounded[1], value_weight, contract_cols, preferred_element_type=jnp.float32)
    encoder_grad = lax.psum_scatter(encoder_terms, "grp", scatter_dimension=1, tiled=True).astype(
        jnp.bfloat16
    )
    both_grads = jnp.concatenate([rounded[0], rounded[1]], 1)
    group_grads = lax.all_gather(both_grads, "byx", axis=0, tiled=True)
    rows = encoder.shape[0]
    slice_rows = model // (outer * inner)
    picked = lax.dynamic_slice_in_dim(
        near.reshape(inner * rows, outer, inner, slice_rows),
        lax.axis_index("byx"),
        1,
        axis=2,
    ).reshape(inner * rows, outer * slice_rows)
    partial = lax.dot_general(
        picked, group_grads, (((0,), (0,)), ((), ())), preferred_element_type=jnp.float32
    )
    weight_rows = lax.psum_scatter(partial, "bz", scatter_dimension=0, tiled=True)
    return (
        attended,
        query_grad,
        encoder_grad,
        weight_rows[:, :head_cols],
        weight_rows[:, head_cols:],
    )


def solution(mesh):
    blk_size, grp_size = mesh.devices.shape
    outer = 4 if blk_size % 4 == 0 else 1
    inner = blk_size // outer
    split = jax.sharding.Mesh(
        mesh.devices.reshape(outer, inner, grp_size), ("bz", "byx", "grp")
    )
    blk = ("bz", "byx")
    in_specs = (
        P(blk, "grp"),
        P(blk, None),
        P(None, "grp"),
        P(None, "grp"),
        P(blk, "grp"),
        P(blk, None),
        P(blk),
    )
    out_specs = (
        P(blk, "grp"),
        P(blk, "grp"),
        P(blk, "grp"),
        P(blk, "grp"),
        P(blk, "grp"),
    )
    return jax.shard_map(
        functools.partial(on_device, outer=outer, inner=inner),
        mesh=split,
        in_specs=in_specs,
        out_specs=out_specs,
        check_vma=False,
    )
```

```python
import functools

import jax
import jax.numpy as jnp
from jax import lax
from jax.experimental import pallas as pl
from jax.experimental.pallas import tpu as pltpu
from jax.sharding import PartitionSpec as P

HEAD_DIM = 64
REACH = 4
LISTED = 5
LANES = 128


def passed_along(value, axis, by, size):
    pairs = [(i, i + by) for i in range(size) if 0 <= i + by < size]
    return lax.ppermute(value, axis, pairs)


def attention_kernel(slots_ref, counts_ref, q_ref, g_ref, stock_ref, out_ref, dq_ref, acc_ref):
    factor = HEAD_DIM ** (-0.5)
    step = pl.program_id(0)

    @pl.when(step == 0)
    def _():
        acc_ref[...] = jnp.zeros_like(acc_ref)

    count = counts_ref[step]
    rows = q_ref.shape[0]
    lane = lax.broadcasted_iota(jnp.int32, (rows, LANES), 1)
    first = lane < HEAD_DIM
    slots = [slots_ref[step, j] for j in range(LISTED)]
    nt = (((1,), (1,)), ((), ()))
    tn = (((0,), (0,)), ((), ()))
    f32 = jnp.float32
    bf16 = jnp.bfloat16

    def run(used):
        def pair(p, carry):
            off = pl.multiple_of(p * LANES, LANES)
            qp = q_ref[:, pl.ds(off, LANES)]
            gp = g_ref[:, pl.ds(off, LANES)]
            qs = qp * jnp.asarray(factor, qp.dtype)
            gs = gp * jnp.asarray(factor, gp.dtype)
            zq = jnp.zeros_like(qp)
            qh = [jnp.where(first, qp, zq), jnp.where(first, zq, qp)]
            gh = [jnp.where(first, gp, zq), jnp.where(first, zq, gp)]
            qsh = [jnp.where(first, qs, zq), jnp.where(first, zq, qs)]
            gsh = [jnp.where(first, gs, zq), jnp.where(first, zq, gs)]
            ks = [stock_ref[slots[j], 0, :, pl.ds(off, LANES)] for j in range(used)]
            vs = [stock_ref[slots[j], 1, :, pl.ds(off, LANES)] for j in range(used)]
            outs, dqs = [], []
            dks = [None] * used
            dvs = [None] * used
            for h in range(2):
                scores = [
                    lax.dot_general(qsh[h], ks[j], nt, preferred_element_type=f32)
                    for j in range(used)
                ]
                peak = jnp.max(scores[0], axis=1, keepdims=True)
                for j in range(1, used):
                    peak = jnp.maximum(peak, jnp.max(scores[j], axis=1, keepdims=True))
                expos = [jnp.exp(sc - peak) for sc in scores]
                total = jnp.sum(expos[0], axis=1, keepdims=True)
                for j in range(1, used):
                    total = total + jnp.sum(expos[j], axis=1, keepdims=True)
                inverse = 1.0 / total
                ws = [(e * inverse).astype(bf16) for e in expos]
                out = jnp.dot(ws[0], vs[0], preferred_element_type=f32)
                for j in range(1, used):
                    out = out + jnp.dot(ws[j], vs[j], preferred_element_type=f32)
                dws = [
                    lax.dot_general(gsh[h], vs[j], nt, preferred_element_type=f32)
                    for j in range(used)
                ]
                wf = [w.astype(f32) for w in ws]
                center = jnp.sum(wf[0] * dws[0], axis=1, keepdims=True)
                for j in range(1, used):
                    center = center + jnp.sum(wf[j] * dws[j], axis=1, keepdims=True)
                dss = [(wf[j] * (dws[j] - center)).astype(bf16) for j in range(used)]
                dq = jnp.dot(dss[0], ks[0], preferred_element_type=f32)
                for j in range(1, used):
                    dq = dq + jnp.dot(dss[j], ks[j], preferred_element_type=f32)
                for j in range(used):
                    dk = lax.dot_general(dss[j], qh[h], tn, preferred_element_type=f32)
                    dv = lax.dot_general(ws[j], gh[h], tn, preferred_element_type=f32)
                    dks[j] = dk if dks[j] is None else dks[j] + dk
                    dvs[j] = dv if dvs[j] is None else dvs[j] + dv
                outs.append(out)
                dqs.append(dq)
            out_ref[:, pl.ds(off, LANES)] = jnp.where(first, outs[0], outs[1]).astype(out_ref.dtype)
            dq_ref[:, pl.ds(off, LANES)] = jnp.where(first, dqs[0], dqs[1]).astype(dq_ref.dtype)
            for j in range(used):
                acc_ref[slots[j], 0, :, pl.ds(off, LANES)] += dks[j]
                acc_ref[slots[j], 1, :, pl.ds(off, LANES)] += dvs[j]
            return carry

        lax.fori_loop(0, q_ref.shape[1] // LANES, pair, 0)

    for used in range(1, LISTED + 1):
        pl.when(count == used)(functools.partial(run, used))


def attention(queries, out_grad, stock, slot_ids, counts):
    rows, cols = stock.shape[2], stock.shape[3]
    blocks = queries.shape[0] // rows
    n_slots = stock.shape[0]
    flops = blocks * (cols // LANES) * 2 * LISTED * 6 * 2 * rows * LANES * LANES
    bytes_accessed = 4 * queries.size * 2 + stock.size * 2 + stock.size * 4
    grid_spec = pltpu.PrefetchScalarGridSpec(
        num_scalar_prefetch=2,
        grid=(blocks,),
        in_specs=[
            pl.BlockSpec((rows, cols), lambda i, s, c: (i, 0)),
            pl.BlockSpec((rows, cols), lambda i, s, c: (i, 0)),
            pl.BlockSpec((n_slots, 2, rows, cols), lambda i, s, c: (0, 0, 0, 0)),
        ],
        out_specs=[
            pl.BlockSpec((rows, cols), lambda i, s, c: (i, 0)),
            pl.BlockSpec((rows, cols), lambda i, s, c: (i, 0)),
            pl.BlockSpec((n_slots, 2, rows, cols), lambda i, s, c: (0, 0, 0, 0)),
        ],
    )
    return pl.pallas_call(
        attention_kernel,
        grid_spec=grid_spec,
        out_shape=[
            jax.ShapeDtypeStruct(queries.shape, jnp.bfloat16),
            jax.ShapeDtypeStruct(queries.shape, jnp.bfloat16),
            jax.ShapeDtypeStruct(stock.shape, jnp.float32),
        ],
        compiler_params=pltpu.CompilerParams(dimension_semantics=("arbitrary",)),
        cost_estimate=pl.CostEstimate(
            flops=flops, transcendentals=blocks * rows * LISTED * rows * (cols // HEAD_DIM),
            bytes_accessed=bytes_accessed,
        ),
    )(slot_ids, counts, queries, out_grad, stock)


def on_device(
    queries, encoder, key_weight, value_weight, out_grad, block_lists, list_counts, outer, inner
):
    blk = ("bz", "byx")
    position = lax.axis_index(blk)
    head_cols = key_weight.shape[1]
    model = encoder.shape[1]
    near = lax.all_gather(encoder, "byx", axis=0, tiled=False)
    own_keys = jnp.dot(encoder, key_weight, preferred_element_type=jnp.float32).astype(jnp.bfloat16)
    own_values = jnp.dot(encoder, value_weight, preferred_element_type=jnp.float32).astype(
        jnp.bfloat16
    )
    own = jnp.stack([own_keys, own_values], 0)
    arrived = []
    for offset in range(-REACH, REACH + 1):
        if offset == 0:
            arrived.append(own)
        else:
            arrived.append(passed_along(own, blk, -offset, outer * inner))
    stock = jnp.stack(arrived, 0)
    slot_ids = (block_lists - (position - REACH)).astype(jnp.int32)
    attended, query_grad, running = attention(
        queries, out_grad, stock, slot_ids, list_counts.astype(jnp.int32)
    )
    owned = running[REACH]
    for offset in range(-REACH, REACH + 1):
        if offset != 0:
            owned = owned + passed_along(running[REACH + offset], blk, offset, outer * inner)
    rounded = owned.astype(jnp.bfloat16)
    contract_cols = (((1,), (1,)), ((), ()))
    encoder_terms = lax.dot_general(
        rounded[0], key_weight, contract_cols, preferred_element_type=jnp.float32
    ) + lax.dot_general(rounded[1], value_weight, contract_cols, preferred_element_type=jnp.float32)
    encoder_grad = lax.psum_scatter(encoder_terms, "grp", scatter_dimension=1, tiled=True).astype(
        jnp.bfloat16
    )
    both_grads = jnp.concatenate([rounded[0], rounded[1]], 1)
    group_grads = lax.all_gather(both_grads, "byx", axis=0, tiled=True)
    rows = encoder.shape[0]
    slice_rows = model // (outer * inner)
    picked = lax.dynamic_slice_in_dim(
        near.reshape(inner * rows, outer, inner, slice_rows),
        lax.axis_index("byx"),
        1,
        axis=2,
    ).reshape(inner * rows, outer * slice_rows)
    partial = lax.dot_general(
        picked, group_grads, (((0,), (0,)), ((), ())), preferred_element_type=jnp.float32
    )
    weight_rows = lax.psum_scatter(partial, "bz", scatter_dimension=0, tiled=True)
    return (
        attended,
        query_grad,
        encoder_grad,
        weight_rows[:, :head_cols],
        weight_rows[:, head_cols:],
    )


def solution(mesh):
    blk_size, grp_size = mesh.devices.shape
    outer = 4 if blk_size % 4 == 0 else 1
    inner = blk_size // outer
    split = jax.sharding.Mesh(
        mesh.devices.reshape(outer, inner, grp_size), ("bz", "byx", "grp")
    )
    blk = ("bz", "byx")
    in_specs = (
        P(blk, "grp"),
        P(blk, None),
        P(None, "grp"),
        P(None, "grp"),
        P(blk, "grp"),
        P(blk, None),
        P(blk),
    )
    out_specs = (
        P(blk, "grp"),
        P(blk, "grp"),
        P(blk, "grp"),
        P(blk, "grp"),
        P(blk, "grp"),
    )
    return jax.shard_map(
        functools.partial(on_device, outer=outer, inner=inner),
        mesh=split,
        in_specs=in_specs,
        out_specs=out_specs,
        check_vma=False,
    )
```

```python
import functools

import jax
import jax.numpy as jnp
from jax import lax
from jax.experimental import pallas as pl
from jax.experimental.pallas import tpu as pltpu
from jax.sharding import PartitionSpec as P

HEAD_DIM = 64
REACH = 4
LISTED = 5
LANES = 128


def passed_along(value, axis, by, size):
    pairs = [(i, i + by) for i in range(size) if 0 <= i + by < size]
    return lax.ppermute(value, axis, pairs)


def attention_kernel(
    slots_ref, counts_ref, q_ref, g_ref, stock_ref, flipped_ref, out_ref, dq_ref, acc_ref
):
    factor = HEAD_DIM ** (-0.5)
    step = pl.program_id(0)

    @pl.when(step == 0)
    def _():
        acc_ref[...] = jnp.zeros_like(acc_ref)

    count = counts_ref[step]
    rows = q_ref.shape[0]
    lane = lax.broadcasted_iota(jnp.int32, (rows, LANES), 1)
    first = lane < HEAD_DIM
    row = lax.broadcasted_iota(jnp.int32, (LANES, rows), 0)
    top = row < HEAD_DIM
    slots = [slots_ref[step, j] for j in range(LISTED)]
    f32 = jnp.float32
    bf16 = jnp.bfloat16

    def dot(a, b):
        return jnp.dot(a, b, preferred_element_type=f32)

    def run(used):
        def pair(p, carry):
            off = pl.multiple_of(p * LANES, LANES)
            qp = q_ref[:, pl.ds(off, LANES)]
            gp = g_ref[:, pl.ds(off, LANES)]
            qt = qp.astype(f32).T * factor
            gt = gp.astype(f32).T * factor
            zf = jnp.zeros_like(qt)
            qst = [jnp.where(top, qt, zf).astype(bf16), jnp.where(top, zf, qt).astype(bf16)]
            gst = [jnp.where(top, gt, zf).astype(bf16), jnp.where(top, zf, gt).astype(bf16)]
            zq = jnp.zeros_like(qp)
            qh = [jnp.where(first, qp, zq), jnp.where(first, zq, qp)]
            gh = [jnp.where(first, gp, zq), jnp.where(first, zq, gp)]
            ks = [stock_ref[slots[j], 0, :, pl.ds(off, LANES)] for j in range(used)]
            vs = [stock_ref[slots[j], 1, :, pl.ds(off, LANES)] for j in range(used)]
            kts = [flipped_ref[slots[j], 0, pl.ds(off, LANES), :] for j in range(used)]
            vts = [flipped_ref[slots[j], 1, pl.ds(off, LANES), :] for j in range(used)]
            outs, dqs = [], []
            dks = [None] * used
            dvs = [None] * used
            for h in range(2):
                scores = [dot(ks[j], qst[h]) for j in range(used)]
                peak = jnp.max(scores[0], axis=0, keepdims=True)
                for j in range(1, used):
                    peak = jnp.maximum(peak, jnp.max(scores[j], axis=0, keepdims=True))
                expos = [jnp.exp(sc - peak) for sc in scores]
                total = jnp.sum(expos[0], axis=0, keepdims=True)
                for j in range(1, used):
                    total = total + jnp.sum(expos[j], axis=0, keepdims=True)
                inverse = 1.0 / total
                ws = [(e * inverse).astype(bf16) for e in expos]
                out = dot(vts[0], ws[0])
                for j in range(1, used):
                    out = out + dot(vts[j], ws[j])
                dws = [dot(vs[j], gst[h]) for j in range(used)]
                wf = [w.astype(f32) for w in ws]
                center = jnp.sum(wf[0] * dws[0], axis=0, keepdims=True)
                for j in range(1, used):
                    center = center + jnp.sum(wf[j] * dws[j], axis=0, keepdims=True)
                dss = [(wf[j] * (dws[j] - center)).astype(bf16) for j in range(used)]
                dq = dot(kts[0], dss[0])
                for j in range(1, used):
                    dq = dq + dot(kts[j], dss[j])
                for j in range(used):
                    dk = dot(dss[j], qh[h])
                    dv = dot(ws[j], gh[h])
                    dks[j] = dk if dks[j] is None else dks[j] + dk
                    dvs[j] = dv if dvs[j] is None else dvs[j] + dv
                outs.append(out)
                dqs.append(dq)
            out_ref[:, pl.ds(off, LANES)] = jnp.where(top, outs[0], outs[1]).T.astype(out_ref.dtype)
            dq_ref[:, pl.ds(off, LANES)] = jnp.where(top, dqs[0], dqs[1]).T.astype(dq_ref.dtype)
            for j in range(used):
                acc_ref[slots[j], 0, :, pl.ds(off, LANES)] += dks[j]
                acc_ref[slots[j], 1, :, pl.ds(off, LANES)] += dvs[j]
            return carry

        lax.fori_loop(0, q_ref.shape[1] // LANES, pair, 0)

    for used in range(1, LISTED + 1):
        pl.when(count == used)(functools.partial(run, used))


def attention(queries, out_grad, stock, slot_ids, counts):
    rows, cols = stock.shape[2], stock.shape[3]
    blocks = queries.shape[0] // rows
    n_slots = stock.shape[0]
    flipped = jnp.swapaxes(stock, 2, 3)
    flops = blocks * (cols // LANES) * 2 * 3 * 6 * 2 * rows * LANES * LANES
    bytes_accessed = 4 * queries.size * 2 + 2 * stock.size * 2 + stock.size * 4
    grid_spec = pltpu.PrefetchScalarGridSpec(
        num_scalar_prefetch=2,
        grid=(blocks,),
        in_specs=[
            pl.BlockSpec((rows, cols), lambda i, s, c: (i, 0)),
            pl.BlockSpec((rows, cols), lambda i, s, c: (i, 0)),
            pl.BlockSpec((n_slots, 2, rows, cols), lambda i, s, c: (0, 0, 0, 0)),
            pl.BlockSpec((n_slots, 2, cols, rows), lambda i, s, c: (0, 0, 0, 0)),
        ],
        out_specs=[
            pl.BlockSpec((rows, cols), lambda i, s, c: (i, 0)),
            pl.BlockSpec((rows, cols), lambda i, s, c: (i, 0)),
            pl.BlockSpec((n_slots, 2, rows, cols), lambda i, s, c: (0, 0, 0, 0)),
        ],
    )
    return pl.pallas_call(
        attention_kernel,
        grid_spec=grid_spec,
        out_shape=[
            jax.ShapeDtypeStruct(queries.shape, jnp.bfloat16),
            jax.ShapeDtypeStruct(queries.shape, jnp.bfloat16),
            jax.ShapeDtypeStruct(stock.shape, jnp.float32),
        ],
        compiler_params=pltpu.CompilerParams(dimension_semantics=("arbitrary",)),
        cost_estimate=pl.CostEstimate(
            flops=flops, transcendentals=blocks * rows * 3 * rows * (cols // HEAD_DIM),
            bytes_accessed=bytes_accessed,
        ),
    )(slot_ids, counts, queries, out_grad, stock, flipped)


def on_device(
    queries, encoder, key_weight, value_weight, out_grad, block_lists, list_counts, outer, inner
):
    blk = ("bz", "byx")
    position = lax.axis_index(blk)
    head_cols = key_weight.shape[1]
    model = encoder.shape[1]
    near = lax.all_gather(encoder, "byx", axis=0, tiled=False)
    own_keys = jnp.dot(encoder, key_weight, preferred_element_type=jnp.float32).astype(jnp.bfloat16)
    own_values = jnp.dot(encoder, value_weight, preferred_element_type=jnp.float32).astype(
        jnp.bfloat16
    )
    own = jnp.stack([own_keys, own_values], 0)
    arrived = []
    for offset in range(-REACH, REACH + 1):
        if offset == 0:
            arrived.append(own)
        else:
            arrived.append(passed_along(own, blk, -offset, outer * inner))
    stock = jnp.stack(arrived, 0)
    slot_ids = (block_lists - (position - REACH)).astype(jnp.int32)
    attended, query_grad, running = attention(
        queries, out_grad, stock, slot_ids, list_counts.astype(jnp.int32)
    )
    owned = running[REACH]
    for offset in range(-REACH, REACH + 1):
        if offset != 0:
            owned = owned + passed_along(running[REACH + offset], blk, offset, outer * inner)
    rounded = owned.astype(jnp.bfloat16)
    contract_cols = (((1,), (1,)), ((), ()))
    encoder_terms = lax.dot_general(
        rounded[0], key_weight, contract_cols, preferred_element_type=jnp.float32
    ) + lax.dot_general(rounded[1], value_weight, contract_cols, preferred_element_type=jnp.float32)
    encoder_grad = lax.psum_scatter(encoder_terms, "grp", scatter_dimension=1, tiled=True).astype(
        jnp.bfloat16
    )
    both_grads = jnp.concatenate([rounded[0], rounded[1]], 1)
    group_grads = lax.all_gather(both_grads, "byx", axis=0, tiled=True)
    rows = encoder.shape[0]
    slice_rows = model // (outer * inner)
    picked = lax.dynamic_slice_in_dim(
        near.reshape(inner * rows, outer, inner, slice_rows),
        lax.axis_index("byx"),
        1,
        axis=2,
    ).reshape(inner * rows, outer * slice_rows)
    partial = lax.dot_general(
        picked, group_grads, (((0,), (0,)), ((), ())), preferred_element_type=jnp.float32
    )
    weight_rows = lax.psum_scatter(partial, "bz", scatter_dimension=0, tiled=True)
    return (
        attended,
        query_grad,
        encoder_grad,
        weight_rows[:, :head_cols],
        weight_rows[:, head_cols:],
    )


def solution(mesh):
    blk_size, grp_size = mesh.devices.shape
    outer = 4 if blk_size % 4 == 0 else 1
    inner = blk_size // outer
    split = jax.sharding.Mesh(
        mesh.devices.reshape(outer, inner, grp_size), ("bz", "byx", "grp")
    )
    blk = ("bz", "byx")
    in_specs = (
        P(blk, "grp"),
        P(blk, None),
        P(None, "grp"),
        P(None, "grp"),
        P(blk, "grp"),
        P(blk, None),
        P(blk),
    )
    out_specs = (
        P(blk, "grp"),
        P(blk, "grp"),
        P(blk, "grp"),
        P(blk, "grp"),
        P(blk, "grp"),
    )
    return jax.shard_map(
        functools.partial(on_device, outer=outer, inner=inner),
        mesh=split,
        in_specs=in_specs,
        out_specs=out_specs,
        check_vma=False,
    )
```

```python
import functools

import jax
import jax.numpy as jnp
from jax import lax
from jax.experimental import pallas as pl
from jax.experimental.pallas import tpu as pltpu
from jax.sharding import PartitionSpec as P

HEAD_DIM = 64
REACH = 4
LISTED = 5
LANES = 128


def passed_along(value, axis, by, size):
    pairs = [(i, i + by) for i in range(size) if 0 <= i + by < size]
    return lax.ppermute(value, axis, pairs)


def attention_kernel(
    slots_ref, counts_ref, q_ref, g_ref, stock_ref, flipped_ref, out_ref, dq_ref, acc_ref
):
    factor = HEAD_DIM ** (-0.5)
    step = pl.program_id(0)

    @pl.when(step == 0)
    def _():
        acc_ref[...] = jnp.zeros_like(acc_ref)

    count = counts_ref[step]
    rows = q_ref.shape[0]
    lane = lax.broadcasted_iota(jnp.int32, (rows, LANES), 1)
    first = lane < HEAD_DIM
    row = lax.broadcasted_iota(jnp.int32, (LANES, rows), 0)
    top = row < HEAD_DIM
    slots = [slots_ref[step, j] for j in range(LISTED)]
    f32 = jnp.float32
    bf16 = jnp.bfloat16

    def dot(a, b):
        return jnp.dot(a, b, preferred_element_type=f32)

    def run(used):
        def pair(p, carry):
            off = pl.multiple_of(p * LANES, LANES)
            qp = q_ref[:, pl.ds(off, LANES)]
            gp = g_ref[:, pl.ds(off, LANES)]
            qt = qp.astype(f32).T * factor
            gt = gp.astype(f32).T * factor
            zf = jnp.zeros_like(qt)
            qst = [jnp.where(top, qt, zf).astype(bf16), jnp.where(top, zf, qt).astype(bf16)]
            gst = [jnp.where(top, gt, zf).astype(bf16), jnp.where(top, zf, gt).astype(bf16)]
            zq = jnp.zeros_like(qp)
            qh = [jnp.where(first, qp, zq), jnp.where(first, zq, qp)]
            gh = [jnp.where(first, gp, zq), jnp.where(first, zq, gp)]
            ks = [stock_ref[slots[j], 0, :, pl.ds(off, LANES)] for j in range(used)]
            vs = [stock_ref[slots[j], 1, :, pl.ds(off, LANES)] for j in range(used)]
            kts = [flipped_ref[slots[j], 0, pl.ds(off, LANES), :] for j in range(used)]
            vts = [flipped_ref[slots[j], 1, pl.ds(off, LANES), :] for j in range(used)]
            outs, dqs = [], []
            dks = [None] * used
            dvs = [None] * used
            for h in range(2):
                scores = [dot(ks[j], qst[h]) for j in range(used)]
                peak = jnp.max(scores[0], axis=0, keepdims=True)
                for j in range(1, used):
                    peak = jnp.maximum(peak, jnp.max(scores[j], axis=0, keepdims=True))
                expos = [jnp.exp(sc - peak) for sc in scores]
                total = jnp.sum(expos[0], axis=0, keepdims=True)
                for j in range(1, used):
                    total = total + jnp.sum(expos[j], axis=0, keepdims=True)
                inverse = 1.0 / total
                ws = [(e * inverse).astype(bf16) for e in expos]
                out = dot(vts[0], ws[0])
                for j in range(1, used):
                    out = out + dot(vts[j], ws[j])
                dws = [dot(vs[j], gst[h]) for j in range(used)]
                wf = [w.astype(f32) for w in ws]
                center = jnp.sum(wf[0] * dws[0], axis=0, keepdims=True)
                for j in range(1, used):
                    center = center + jnp.sum(wf[j] * dws[j], axis=0, keepdims=True)
                dss = [(wf[j] * (dws[j] - center)).astype(bf16) for j in range(used)]
                dq = dot(kts[0], dss[0])
                for j in range(1, used):
                    dq = dq + dot(kts[j], dss[j])
                for j in range(used):
                    dk = dot(dss[j], qh[h])
                    dv = dot(ws[j], gh[h])
                    dks[j] = dk if dks[j] is None else dks[j] + dk
                    dvs[j] = dv if dvs[j] is None else dvs[j] + dv
                outs.append(out)
                dqs.append(dq)
            out_ref[:, pl.ds(off, LANES)] = jnp.where(top, outs[0], outs[1]).T.astype(out_ref.dtype)
            dq_ref[:, pl.ds(off, LANES)] = jnp.where(top, dqs[0], dqs[1]).T.astype(dq_ref.dtype)
            for j in range(used):
                acc_ref[slots[j], 0, :, pl.ds(off, LANES)] += dks[j]
                acc_ref[slots[j], 1, :, pl.ds(off, LANES)] += dvs[j]
            return carry

        lax.fori_loop(0, q_ref.shape[1] // LANES, pair, 0)

    for used in range(1, LISTED + 1):
        pl.when(count == used)(functools.partial(run, used))


def attention(queries, out_grad, stock, slot_ids, counts):
    rows, cols = stock.shape[2], stock.shape[3]
    blocks = queries.shape[0] // rows
    n_slots = stock.shape[0]
    flipped = jnp.swapaxes(stock, 2, 3)
    flops = blocks * (cols // LANES) * 2 * 3 * 6 * 2 * rows * LANES * LANES
    bytes_accessed = 4 * queries.size * 2 + 2 * stock.size * 2 + stock.size * 4
    grid_spec = pltpu.PrefetchScalarGridSpec(
        num_scalar_prefetch=2,
        grid=(blocks,),
        in_specs=[
            pl.BlockSpec((rows, cols), lambda i, s, c: (i, 0)),
            pl.BlockSpec((rows, cols), lambda i, s, c: (i, 0)),
            pl.BlockSpec((n_slots, 2, rows, cols), lambda i, s, c: (0, 0, 0, 0)),
            pl.BlockSpec((n_slots, 2, cols, rows), lambda i, s, c: (0, 0, 0, 0)),
        ],
        out_specs=[
            pl.BlockSpec((rows, cols), lambda i, s, c: (i, 0)),
            pl.BlockSpec((rows, cols), lambda i, s, c: (i, 0)),
            pl.BlockSpec((n_slots, 2, rows, cols), lambda i, s, c: (0, 0, 0, 0)),
        ],
    )
    return pl.pallas_call(
        attention_kernel,
        grid_spec=grid_spec,
        out_shape=[
            jax.ShapeDtypeStruct(queries.shape, jnp.bfloat16),
            jax.ShapeDtypeStruct(queries.shape, jnp.bfloat16),
            jax.ShapeDtypeStruct(stock.shape, jnp.float32),
        ],
        compiler_params=pltpu.CompilerParams(dimension_semantics=("arbitrary",)),
        cost_estimate=pl.CostEstimate(
            flops=flops, transcendentals=blocks * rows * 3 * rows * (cols // HEAD_DIM),
            bytes_accessed=bytes_accessed,
        ),
    )(slot_ids, counts, queries, out_grad, stock, flipped)


def on_device(
    queries, encoder, key_weight, value_weight, out_grad, block_lists, list_counts, outer, inner
):
    blk = ("bz", "byx")
    position = lax.axis_index(blk)
    head_cols = key_weight.shape[1]
    model = encoder.shape[1]
    near = lax.all_gather(encoder, "byx", axis=0, tiled=False)
    own_keys = jnp.dot(encoder, key_weight, preferred_element_type=jnp.float32).astype(jnp.bfloat16)
    own_values = jnp.dot(encoder, value_weight, preferred_element_type=jnp.float32).astype(
        jnp.bfloat16
    )
    own = jnp.stack([own_keys, own_values], 0)
    arrived = []
    for offset in range(-REACH, REACH + 1):
        if offset == 0:
            arrived.append(own)
        else:
            arrived.append(passed_along(own, blk, -offset, outer * inner))
    stock = jnp.stack(arrived, 0)
    slot_ids = (block_lists - (position - REACH)).astype(jnp.int32)
    attended, query_grad, running = attention(
        queries, out_grad, stock, slot_ids, list_counts.astype(jnp.int32)
    )
    owned = running[REACH]
    for offset in range(-REACH, REACH + 1):
        if offset != 0:
            sent = running[REACH + offset].astype(jnp.bfloat16)
            owned = owned + passed_along(sent, blk, offset, outer * inner).astype(jnp.float32)
    rounded = owned.astype(jnp.bfloat16)
    contract_cols = (((1,), (1,)), ((), ()))
    encoder_terms = lax.dot_general(
        rounded[0], key_weight, contract_cols, preferred_element_type=jnp.float32
    ) + lax.dot_general(rounded[1], value_weight, contract_cols, preferred_element_type=jnp.float32)
    encoder_grad = lax.psum_scatter(encoder_terms, "grp", scatter_dimension=1, tiled=True).astype(
        jnp.bfloat16
    )
    both_grads = jnp.concatenate([rounded[0], rounded[1]], 1)
    group_grads = lax.all_gather(both_grads, "byx", axis=0, tiled=True)
    rows = encoder.shape[0]
    slice_rows = model // (outer * inner)
    picked = lax.dynamic_slice_in_dim(
        near.reshape(inner * rows, outer, inner, slice_rows),
        lax.axis_index("byx"),
        1,
        axis=2,
    ).reshape(inner * rows, outer * slice_rows)
    partial = lax.dot_general(
        picked, group_grads, (((0,), (0,)), ((), ())), preferred_element_type=jnp.float32
    )
    weight_rows = lax.psum_scatter(partial, "bz", scatter_dimension=0, tiled=True)
    return (
        attended,
        query_grad,
        encoder_grad,
        weight_rows[:, :head_cols],
        weight_rows[:, head_cols:],
    )


def solution(mesh):
    blk_size, grp_size = mesh.devices.shape
    outer = 4 if blk_size % 4 == 0 else 1
    inner = blk_size // outer
    split = jax.sharding.Mesh(
        mesh.devices.reshape(outer, inner, grp_size), ("bz", "byx", "grp")
    )
    blk = ("bz", "byx")
    in_specs = (
        P(blk, "grp"),
        P(blk, None),
        P(None, "grp"),
        P(None, "grp"),
        P(blk, "grp"),
        P(blk, None),
        P(blk),
    )
    out_specs = (
        P(blk, "grp"),
        P(blk, "grp"),
        P(blk, "grp"),
        P(blk, "grp"),
        P(blk, "grp"),
    )
    return jax.shard_map(
        functools.partial(on_device, outer=outer, inner=inner),
        mesh=split,
        in_specs=in_specs,
        out_specs=out_specs,
        check_vma=False,
    )
```

```python
import functools

import jax
import jax.numpy as jnp
from jax import lax
from jax.experimental import pallas as pl
from jax.experimental.pallas import tpu as pltpu
from jax.sharding import PartitionSpec as P

HEAD_DIM = 64
REACH = 4
LISTED = 5
LANES = 128


def passed_along(value, axis, by, size):
    pairs = [(i, i + by) for i in range(size) if 0 <= i + by < size]
    return lax.ppermute(value, axis, pairs)


def attention_kernel(
    slots_ref, counts_ref, q_ref, g_ref, stock_ref, flipped_ref, out_ref, dq_ref, acc_ref
):
    factor = HEAD_DIM ** (-0.5)
    step = pl.program_id(0)

    @pl.when(step == 0)
    def _():
        acc_ref[...] = jnp.zeros_like(acc_ref)

    count = counts_ref[step]
    rows = q_ref.shape[0]
    lane = lax.broadcasted_iota(jnp.int32, (rows, LANES), 1)
    first = lane < HEAD_DIM
    row = lax.broadcasted_iota(jnp.int32, (LANES, rows), 0)
    top = row < HEAD_DIM
    slots = [slots_ref[step, j] for j in range(LISTED)]
    f32 = jnp.float32
    bf16 = jnp.bfloat16

    def dot(a, b):
        return jnp.dot(a, b, preferred_element_type=f32)

    def run(used):
        def pair(p, carry):
            off = pl.multiple_of(p * LANES, LANES)
            qp = q_ref[:, pl.ds(off, LANES)]
            gp = g_ref[:, pl.ds(off, LANES)]
            qt = qp.astype(f32).T * factor
            gt = gp.astype(f32).T * factor
            zf = jnp.zeros_like(qt)
            qst = [jnp.where(top, qt, zf).astype(bf16), jnp.where(top, zf, qt).astype(bf16)]
            gst = [jnp.where(top, gt, zf).astype(bf16), jnp.where(top, zf, gt).astype(bf16)]
            zq = jnp.zeros_like(qp)
            qh = [jnp.where(first, qp, zq), jnp.where(first, zq, qp)]
            gh = [jnp.where(first, gp, zq), jnp.where(first, zq, gp)]
            ks = [stock_ref[slots[j], 0, :, pl.ds(off, LANES)] for j in range(used)]
            vs = [stock_ref[slots[j], 1, :, pl.ds(off, LANES)] for j in range(used)]
            kts = [flipped_ref[slots[j], 0, pl.ds(off, LANES), :] for j in range(used)]
            vts = [flipped_ref[slots[j], 1, pl.ds(off, LANES), :] for j in range(used)]
            outs, dqs = [], []
            dks = [None] * used
            dvs = [None] * used
            for h in range(2):
                scores = [dot(ks[j], qst[h]) for j in range(used)]
                peak = jnp.max(scores[0], axis=0, keepdims=True)
                for j in range(1, used):
                    peak = jnp.maximum(peak, jnp.max(scores[j], axis=0, keepdims=True))
                expos = [jnp.exp(sc - peak) for sc in scores]
                total = jnp.sum(expos[0], axis=0, keepdims=True)
                for j in range(1, used):
                    total = total + jnp.sum(expos[j], axis=0, keepdims=True)
                inverse = 1.0 / total
                ws = [(e * inverse).astype(bf16) for e in expos]
                out = dot(vts[0], ws[0])
                for j in range(1, used):
                    out = out + dot(vts[j], ws[j])
                dws = [dot(vs[j], gst[h]) for j in range(used)]
                wf = [w.astype(f32) for w in ws]
                center = jnp.sum(wf[0] * dws[0], axis=0, keepdims=True)
                for j in range(1, used):
                    center = center + jnp.sum(wf[j] * dws[j], axis=0, keepdims=True)
                dss = [(wf[j] * (dws[j] - center)).astype(bf16) for j in range(used)]
                dq = dot(kts[0], dss[0])
                for j in range(1, used):
                    dq = dq + dot(kts[j], dss[j])
                for j in range(used):
                    dk = dot(dss[j], qh[h])
                    dv = dot(ws[j], gh[h])
                    dks[j] = dk if dks[j] is None else dks[j] + dk
                    dvs[j] = dv if dvs[j] is None else dvs[j] + dv
                outs.append(out)
                dqs.append(dq)
            out_ref[:, pl.ds(off, LANES)] = jnp.where(top, outs[0], outs[1]).T.astype(out_ref.dtype)
            dq_ref[:, pl.ds(off, LANES)] = jnp.where(top, dqs[0], dqs[1]).T.astype(dq_ref.dtype)
            for j in range(used):
                acc_ref[slots[j], 0, :, pl.ds(off, LANES)] += dks[j]
                acc_ref[slots[j], 1, :, pl.ds(off, LANES)] += dvs[j]
            return carry

        lax.fori_loop(0, q_ref.shape[1] // LANES, pair, 0)

    for used in range(1, LISTED + 1):
        pl.when(count == used)(functools.partial(run, used))


def attention(queries, out_grad, stock, slot_ids, counts):
    rows, cols = stock.shape[2], stock.shape[3]
    blocks = queries.shape[0] // rows
    n_slots = stock.shape[0]
    flipped = jnp.swapaxes(stock, 2, 3)
    flops = blocks * (cols // LANES) * 2 * 3 * 6 * 2 * rows * LANES * LANES
    bytes_accessed = 4 * queries.size * 2 + 2 * stock.size * 2 + stock.size * 4
    grid_spec = pltpu.PrefetchScalarGridSpec(
        num_scalar_prefetch=2,
        grid=(blocks,),
        in_specs=[
            pl.BlockSpec((rows, cols), lambda i, s, c: (i, 0)),
            pl.BlockSpec((rows, cols), lambda i, s, c: (i, 0)),
            pl.BlockSpec((n_slots, 2, rows, cols), lambda i, s, c: (0, 0, 0, 0)),
            pl.BlockSpec((n_slots, 2, cols, rows), lambda i, s, c: (0, 0, 0, 0)),
        ],
        out_specs=[
            pl.BlockSpec((rows, cols), lambda i, s, c: (i, 0)),
            pl.BlockSpec((rows, cols), lambda i, s, c: (i, 0)),
            pl.BlockSpec((n_slots, 2, rows, cols), lambda i, s, c: (0, 0, 0, 0)),
        ],
    )
    return pl.pallas_call(
        attention_kernel,
        grid_spec=grid_spec,
        out_shape=[
            jax.ShapeDtypeStruct(queries.shape, jnp.bfloat16),
            jax.ShapeDtypeStruct(queries.shape, jnp.bfloat16),
            jax.ShapeDtypeStruct(stock.shape, jnp.float32),
        ],
        compiler_params=pltpu.CompilerParams(dimension_semantics=("arbitrary",)),
        cost_estimate=pl.CostEstimate(
            flops=flops, transcendentals=blocks * rows * 3 * rows * (cols // HEAD_DIM),
            bytes_accessed=bytes_accessed,
        ),
    )(slot_ids, counts, queries, out_grad, stock, flipped)


def on_device(queries, encoder, key_weight, value_weight, out_grad, block_lists, list_counts, size):
    blk = ("bz", "by", "bx")
    position = lax.axis_index(blk)
    head_cols = key_weight.shape[1]
    rows, model = encoder.shape
    column = lax.all_gather(encoder, "bz", axis=0, tiled=True)
    own_keys = jnp.dot(encoder, key_weight, preferred_element_type=jnp.float32).astype(jnp.bfloat16)
    own_values = jnp.dot(encoder, value_weight, preferred_element_type=jnp.float32).astype(
        jnp.bfloat16
    )
    own = jnp.stack([own_keys, own_values], 0)
    arrived = []
    for offset in range(-REACH, REACH + 1):
        if offset == 0:
            arrived.append(own)
        else:
            arrived.append(passed_along(own, blk, -offset, size))
    stock = jnp.stack(arrived, 0)
    slot_ids = (block_lists - (position - REACH)).astype(jnp.int32)
    attended, query_grad, running = attention(
        queries, out_grad, stock, slot_ids, list_counts.astype(jnp.int32)
    )
    owned = running[REACH]
    for offset in range(-REACH, REACH + 1):
        if offset != 0:
            sent = running[REACH + offset].astype(jnp.bfloat16)
            owned = owned + passed_along(sent, blk, offset, size).astype(jnp.float32)
    rounded = owned.astype(jnp.bfloat16)
    contract_cols = (((1,), (1,)), ((), ()))
    encoder_terms = lax.dot_general(
        rounded[0], key_weight, contract_cols, preferred_element_type=jnp.float32
    ) + lax.dot_general(rounded[1], value_weight, contract_cols, preferred_element_type=jnp.float32)
    encoder_grad = lax.psum_scatter(encoder_terms, "grp", scatter_dimension=1, tiled=True).astype(
        jnp.bfloat16
    )
    both_grads = jnp.concatenate([rounded[0], rounded[1]], 1)
    column_grads = lax.all_gather(both_grads, "bz", axis=0, tiled=True)
    span = model // (column.shape[0] // rows)
    picked = lax.dynamic_slice_in_dim(column, lax.axis_index("bz") * span, span, axis=1)
    partial = lax.dot_general(
        picked, column_grads, (((0,), (0,)), ((), ())), preferred_element_type=jnp.float32
    )
    partial = lax.psum_scatter(partial, "by", scatter_dimension=0, tiled=True)
    weight_rows = lax.psum_scatter(partial, "bx", scatter_dimension=0, tiled=True)
    return (
        attended,
        query_grad,
        encoder_grad,
        weight_rows[:, :head_cols],
        weight_rows[:, head_cols:],
    )


def solution(mesh):
    blk_size, grp_size = mesh.devices.shape
    split = jax.sharding.Mesh(
        mesh.devices.reshape(4, blk_size // 8, 2, grp_size), ("bz", "by", "bx", "grp")
    )
    blk = ("bz", "by", "bx")
    in_specs = (
        P(blk, "grp"),
        P(blk, None),
        P(None, "grp"),
        P(None, "grp"),
        P(blk, "grp"),
        P(blk, None),
        P(blk),
    )
    out_specs = (
        P(blk, "grp"),
        P(blk, "grp"),
        P(blk, "grp"),
        P(blk, "grp"),
        P(blk, "grp"),
    )
    return jax.shard_map(
        functools.partial(on_device, size=blk_size),
        mesh=split,
        in_specs=in_specs,
        out_specs=out_specs,
        check_vma=False,
    )
```

```python
import functools

import jax
import jax.numpy as jnp
from jax import lax
from jax.experimental import pallas as pl
from jax.experimental.pallas import tpu as pltpu
from jax.sharding import PartitionSpec as P

HEAD_DIM = 64
REACH = 4
LISTED = 5
LANES = 128


def passed_along(value, axis, by, size):
    pairs = [(i, i + by) for i in range(size) if 0 <= i + by < size]
    return lax.ppermute(value, axis, pairs)


def attention_kernel(
    slots_ref, counts_ref, q_ref, g_ref, stock_ref, flipped_ref, out_ref, dq_ref, acc_ref
):
    factor = HEAD_DIM ** (-0.5)
    step = pl.program_id(0)

    @pl.when(step == 0)
    def _():
        acc_ref[...] = jnp.zeros_like(acc_ref)

    count = counts_ref[step]
    rows = q_ref.shape[0]
    lane = lax.broadcasted_iota(jnp.int32, (rows, LANES), 1)
    first = lane < HEAD_DIM
    row = lax.broadcasted_iota(jnp.int32, (LANES, rows), 0)
    top = row < HEAD_DIM
    slots = [slots_ref[step, j] for j in range(LISTED)]
    f32 = jnp.float32
    bf16 = jnp.bfloat16

    def dot(a, b):
        return jnp.dot(a, b, preferred_element_type=f32)

    def run(used):
        def pair(p, carry):
            off = pl.multiple_of(p * LANES, LANES)
            qp = q_ref[:, pl.ds(off, LANES)]
            gp = g_ref[:, pl.ds(off, LANES)]
            qt = qp.astype(f32).T * factor
            gt = gp.astype(f32).T * factor
            zf = jnp.zeros_like(qt)
            qst = [jnp.where(top, qt, zf).astype(bf16), jnp.where(top, zf, qt).astype(bf16)]
            gst = [jnp.where(top, gt, zf).astype(bf16), jnp.where(top, zf, gt).astype(bf16)]
            zq = jnp.zeros_like(qp)
            qh = [jnp.where(first, qp, zq), jnp.where(first, zq, qp)]
            gh = [jnp.where(first, gp, zq), jnp.where(first, zq, gp)]
            ks = [stock_ref[slots[j], 0, :, pl.ds(off, LANES)] for j in range(used)]
            vs = [stock_ref[slots[j], 1, :, pl.ds(off, LANES)] for j in range(used)]
            kts = [flipped_ref[slots[j], 0, pl.ds(off, LANES), :] for j in range(used)]
            vts = [flipped_ref[slots[j], 1, pl.ds(off, LANES), :] for j in range(used)]
            qs2 = jnp.concatenate(qst, axis=1)
            gs2 = jnp.concatenate(gst, axis=1)
            q2 = jnp.concatenate(qh, axis=0)
            g2 = jnp.concatenate(gh, axis=0)
            scores = [dot(ks[j], qs2) for j in range(used)]
            peak = jnp.max(scores[0], axis=0, keepdims=True)
            for j in range(1, used):
                peak = jnp.maximum(peak, jnp.max(scores[j], axis=0, keepdims=True))
            expos = [jnp.exp(sc - peak) for sc in scores]
            total = jnp.sum(expos[0], axis=0, keepdims=True)
            for j in range(1, used):
                total = total + jnp.sum(expos[j], axis=0, keepdims=True)
            inverse = 1.0 / total
            ws = [(e * inverse).astype(bf16) for e in expos]
            out = dot(vts[0], ws[0])
            for j in range(1, used):
                out = out + dot(vts[j], ws[j])
            dws = [dot(vs[j], gs2) for j in range(used)]
            wf = [w.astype(f32) for w in ws]
            center = jnp.sum(wf[0] * dws[0], axis=0, keepdims=True)
            for j in range(1, used):
                center = center + jnp.sum(wf[j] * dws[j], axis=0, keepdims=True)
            dss = [(wf[j] * (dws[j] - center)).astype(bf16) for j in range(used)]
            dq = dot(kts[0], dss[0])
            for j in range(1, used):
                dq = dq + dot(kts[j], dss[j])
            dks = [dot(dss[j], q2) for j in range(used)]
            dvs = [dot(ws[j], g2) for j in range(used)]
            out_ref[:, pl.ds(off, LANES)] = jnp.where(
                top, out[:, :rows], out[:, rows:]
            ).T.astype(out_ref.dtype)
            dq_ref[:, pl.ds(off, LANES)] = jnp.where(
                top, dq[:, :rows], dq[:, rows:]
            ).T.astype(dq_ref.dtype)
            for j in range(used):
                acc_ref[slots[j], 0, :, pl.ds(off, LANES)] += dks[j]
                acc_ref[slots[j], 1, :, pl.ds(off, LANES)] += dvs[j]
            return carry

        lax.fori_loop(0, q_ref.shape[1] // LANES, pair, 0)

    for used in range(1, LISTED + 1):
        pl.when(count == used)(functools.partial(run, used))


def attention(queries, out_grad, stock, slot_ids, counts):
    rows, cols = stock.shape[2], stock.shape[3]
    blocks = queries.shape[0] // rows
    n_slots = stock.shape[0]
    flipped = jnp.swapaxes(stock, 2, 3)
    flops = blocks * (cols // LANES) * 2 * 3 * 6 * 2 * rows * LANES * LANES
    bytes_accessed = 4 * queries.size * 2 + 2 * stock.size * 2 + stock.size * 4
    grid_spec = pltpu.PrefetchScalarGridSpec(
        num_scalar_prefetch=2,
        grid=(blocks,),
        in_specs=[
            pl.BlockSpec((rows, cols), lambda i, s, c: (i, 0)),
            pl.BlockSpec((rows, cols), lambda i, s, c: (i, 0)),
            pl.BlockSpec((n_slots, 2, rows, cols), lambda i, s, c: (0, 0, 0, 0)),
            pl.BlockSpec((n_slots, 2, cols, rows), lambda i, s, c: (0, 0, 0, 0)),
        ],
        out_specs=[
            pl.BlockSpec((rows, cols), lambda i, s, c: (i, 0)),
            pl.BlockSpec((rows, cols), lambda i, s, c: (i, 0)),
            pl.BlockSpec((n_slots, 2, rows, cols), lambda i, s, c: (0, 0, 0, 0)),
        ],
    )
    return pl.pallas_call(
        attention_kernel,
        grid_spec=grid_spec,
        out_shape=[
            jax.ShapeDtypeStruct(queries.shape, jnp.bfloat16),
            jax.ShapeDtypeStruct(queries.shape, jnp.bfloat16),
            jax.ShapeDtypeStruct(stock.shape, jnp.float32),
        ],
        compiler_params=pltpu.CompilerParams(dimension_semantics=("arbitrary",)),
        cost_estimate=pl.CostEstimate(
            flops=flops, transcendentals=blocks * rows * 3 * rows * (cols // HEAD_DIM),
            bytes_accessed=bytes_accessed,
        ),
    )(slot_ids, counts, queries, out_grad, stock, flipped)


def on_device(
    queries, encoder, key_weight, value_weight, out_grad, block_lists, list_counts, outer, inner
):
    blk = ("bz", "byx")
    position = lax.axis_index(blk)
    head_cols = key_weight.shape[1]
    model = encoder.shape[1]
    near = lax.all_gather(encoder, "byx", axis=0, tiled=False)
    own_keys = jnp.dot(encoder, key_weight, preferred_element_type=jnp.float32).astype(jnp.bfloat16)
    own_values = jnp.dot(encoder, value_weight, preferred_element_type=jnp.float32).astype(
        jnp.bfloat16
    )
    own = jnp.stack([own_keys, own_values], 0)
    arrived = []
    for offset in range(-REACH, REACH + 1):
        if offset == 0:
            arrived.append(own)
        else:
            arrived.append(passed_along(own, blk, -offset, outer * inner))
    stock = jnp.stack(arrived, 0)
    slot_ids = (block_lists - (position - REACH)).astype(jnp.int32)
    attended, query_grad, running = attention(
        queries, out_grad, stock, slot_ids, list_counts.astype(jnp.int32)
    )
    owned = running[REACH]
    for offset in range(-REACH, REACH + 1):
        if offset != 0:
            sent = running[REACH + offset].astype(jnp.bfloat16)
            owned = owned + passed_along(sent, blk, offset, outer * inner).astype(jnp.float32)
    rounded = owned.astype(jnp.bfloat16)
    contract_cols = (((1,), (1,)), ((), ()))
    encoder_terms = lax.dot_general(
        rounded[0], key_weight, contract_cols, preferred_element_type=jnp.float32
    ) + lax.dot_general(rounded[1], value_weight, contract_cols, preferred_element_type=jnp.float32)
    encoder_grad = lax.psum_scatter(encoder_terms, "grp", scatter_dimension=1, tiled=True).astype(
        jnp.bfloat16
    )
    both_grads = jnp.concatenate([rounded[0], rounded[1]], 1)
    group_grads = lax.all_gather(both_grads, "byx", axis=0, tiled=True)
    rows = encoder.shape[0]
    slice_rows = model // (outer * inner)
    picked = lax.dynamic_slice_in_dim(
        near.reshape(inner * rows, outer, inner, slice_rows),
        lax.axis_index("byx"),
        1,
        axis=2,
    ).reshape(inner * rows, outer * slice_rows)
    partial = lax.dot_general(
        picked, group_grads, (((0,), (0,)), ((), ())), preferred_element_type=jnp.float32
    )
    weight_rows = lax.psum_scatter(partial, "bz", scatter_dimension=0, tiled=True)
    return (
        attended,
        query_grad,
        encoder_grad,
        weight_rows[:, :head_cols],
        weight_rows[:, head_cols:],
    )


def solution(mesh):
    blk_size, grp_size = mesh.devices.shape
    outer = 4 if blk_size % 4 == 0 else 1
    inner = blk_size // outer
    split = jax.sharding.Mesh(
        mesh.devices.reshape(outer, inner, grp_size), ("bz", "byx", "grp")
    )
    blk = ("bz", "byx")
    in_specs = (
        P(blk, "grp"),
        P(blk, None),
        P(None, "grp"),
        P(None, "grp"),
        P(blk, "grp"),
        P(blk, None),
        P(blk),
    )
    out_specs = (
        P(blk, "grp"),
        P(blk, "grp"),
        P(blk, "grp"),
        P(blk, "grp"),
        P(blk, "grp"),
    )
    return jax.shard_map(
        functools.partial(on_device, outer=outer, inner=inner),
        mesh=split,
        in_specs=in_specs,
        out_specs=out_specs,
        check_vma=False,
    )
```

```python
import functools

import jax
import jax.numpy as jnp
from jax import lax
from jax.experimental import pallas as pl
from jax.experimental.pallas import tpu as pltpu
from jax.sharding import PartitionSpec as P

HEAD_DIM = 64
REACH = 4
LISTED = 5
LANES = 128


def passed_along(value, axis, by, size):
    pairs = [(i, i + by) for i in range(size) if 0 <= i + by < size]
    return lax.ppermute(value, axis, pairs)


def attention_kernel(
    slots_ref, counts_ref, q_ref, g_ref, stock_ref, flipped_ref, out_ref, dq_ref, acc_ref
):
    factor = HEAD_DIM ** (-0.5)
    step = pl.program_id(0)

    @pl.when(step == 0)
    def _():
        acc_ref[...] = jnp.zeros_like(acc_ref)

    count = counts_ref[step]
    rows = q_ref.shape[0]
    lane = lax.broadcasted_iota(jnp.int32, (rows, LANES), 1)
    first = lane < HEAD_DIM
    row = lax.broadcasted_iota(jnp.int32, (LANES, rows), 0)
    top = row < HEAD_DIM
    slots = [slots_ref[step, j] for j in range(LISTED)]
    f32 = jnp.float32
    bf16 = jnp.bfloat16

    def dot(a, b):
        return jnp.dot(a, b, preferred_element_type=f32)

    def run(used):
        def pair(p, carry):
            off = pl.multiple_of(p * LANES, LANES)
            qp = q_ref[:, pl.ds(off, LANES)]
            gp = g_ref[:, pl.ds(off, LANES)]
            qt = qp.astype(f32).T * factor
            gt = gp.astype(f32).T * factor
            zf = jnp.zeros_like(qt)
            qst = [jnp.where(top, qt, zf).astype(bf16), jnp.where(top, zf, qt).astype(bf16)]
            gst = [jnp.where(top, gt, zf).astype(bf16), jnp.where(top, zf, gt).astype(bf16)]
            zq = jnp.zeros_like(qp)
            qh = [jnp.where(first, qp, zq), jnp.where(first, zq, qp)]
            gh = [jnp.where(first, gp, zq), jnp.where(first, zq, gp)]
            ks = [stock_ref[slots[j], 0, :, pl.ds(off, LANES)] for j in range(used)]
            vs = [stock_ref[slots[j], 1, :, pl.ds(off, LANES)] for j in range(used)]
            kts = [flipped_ref[slots[j], 0, pl.ds(off, LANES), :] for j in range(used)]
            vts = [flipped_ref[slots[j], 1, pl.ds(off, LANES), :] for j in range(used)]
            outs, dqs = [], []
            dks = [None] * used
            dvs = [None] * used
            for h in range(2):
                scores = [dot(ks[j], qst[h]) for j in range(used)]
                peak = jnp.max(scores[0], axis=0, keepdims=True)
                for j in range(1, used):
                    peak = jnp.maximum(peak, jnp.max(scores[j], axis=0, keepdims=True))
                expos = [jnp.exp(sc - peak) for sc in scores]
                total = jnp.sum(expos[0], axis=0, keepdims=True)
                for j in range(1, used):
                    total = total + jnp.sum(expos[j], axis=0, keepdims=True)
                inverse = 1.0 / total
                ws = [(e * inverse).astype(bf16) for e in expos]
                out = dot(vts[0], ws[0])
                for j in range(1, used):
                    out = out + dot(vts[j], ws[j])
                dws = [dot(vs[j], gst[h]) for j in range(used)]
                wf = [w.astype(f32) for w in ws]
                center = jnp.sum(wf[0] * dws[0], axis=0, keepdims=True)
                for j in range(1, used):
                    center = center + jnp.sum(wf[j] * dws[j], axis=0, keepdims=True)
                dss = [(wf[j] * (dws[j] - center)).astype(bf16) for j in range(used)]
                dq = dot(kts[0], dss[0])
                for j in range(1, used):
                    dq = dq + dot(kts[j], dss[j])
                for j in range(used):
                    dk = dot(dss[j], qh[h])
                    dv = dot(ws[j], gh[h])
                    dks[j] = dk if dks[j] is None else dks[j] + dk
                    dvs[j] = dv if dvs[j] is None else dvs[j] + dv
                outs.append(out)
                dqs.append(dq)
            out_ref[:, pl.ds(off, LANES)] = jnp.where(top, outs[0], outs[1]).T.astype(out_ref.dtype)
            dq_ref[:, pl.ds(off, LANES)] = jnp.where(top, dqs[0], dqs[1]).T.astype(dq_ref.dtype)
            for j in range(used):
                acc_ref[slots[j], 0, :, pl.ds(off, LANES)] += dks[j]
                acc_ref[slots[j], 1, :, pl.ds(off, LANES)] += dvs[j]
            return carry

        lax.fori_loop(0, q_ref.shape[1] // LANES, pair, 0, unroll=True)

    for used in range(1, LISTED + 1):
        pl.when(count == used)(functools.partial(run, used))


def attention(queries, out_grad, stock, slot_ids, counts):
    rows, cols = stock.shape[2], stock.shape[3]
    blocks = queries.shape[0] // rows
    n_slots = stock.shape[0]
    flipped = jnp.swapaxes(stock, 2, 3)
    flops = blocks * (cols // LANES) * 2 * 3 * 6 * 2 * rows * LANES * LANES
    bytes_accessed = 4 * queries.size * 2 + 2 * stock.size * 2 + stock.size * 4
    grid_spec = pltpu.PrefetchScalarGridSpec(
        num_scalar_prefetch=2,
        grid=(blocks,),
        in_specs=[
            pl.BlockSpec((rows, cols), lambda i, s, c: (i, 0)),
            pl.BlockSpec((rows, cols), lambda i, s, c: (i, 0)),
            pl.BlockSpec((n_slots, 2, rows, cols), lambda i, s, c: (0, 0, 0, 0)),
            pl.BlockSpec((n_slots, 2, cols, rows), lambda i, s, c: (0, 0, 0, 0)),
        ],
        out_specs=[
            pl.BlockSpec((rows, cols), lambda i, s, c: (i, 0)),
            pl.BlockSpec((rows, cols), lambda i, s, c: (i, 0)),
            pl.BlockSpec((n_slots, 2, rows, cols), lambda i, s, c: (0, 0, 0, 0)),
        ],
    )
    return pl.pallas_call(
        attention_kernel,
        grid_spec=grid_spec,
        out_shape=[
            jax.ShapeDtypeStruct(queries.shape, jnp.bfloat16),
            jax.ShapeDtypeStruct(queries.shape, jnp.bfloat16),
            jax.ShapeDtypeStruct(stock.shape, jnp.float32),
        ],
        compiler_params=pltpu.CompilerParams(dimension_semantics=("arbitrary",)),
        cost_estimate=pl.CostEstimate(
            flops=flops, transcendentals=blocks * rows * 3 * rows * (cols // HEAD_DIM),
            bytes_accessed=bytes_accessed,
        ),
    )(slot_ids, counts, queries, out_grad, stock, flipped)


def on_device(
    queries, encoder, key_weight, value_weight, out_grad, block_lists, list_counts, outer, inner
):
    blk = ("bz", "byx")
    position = lax.axis_index(blk)
    head_cols = key_weight.shape[1]
    model = encoder.shape[1]
    near = lax.all_gather(encoder, "byx", axis=0, tiled=False)
    own_keys = jnp.dot(encoder, key_weight, preferred_element_type=jnp.float32).astype(jnp.bfloat16)
    own_values = jnp.dot(encoder, value_weight, preferred_element_type=jnp.float32).astype(
        jnp.bfloat16
    )
    own = jnp.stack([own_keys, own_values], 0)
    arrived = []
    for offset in range(-REACH, REACH + 1):
        if offset == 0:
            arrived.append(own)
        else:
            arrived.append(passed_along(own, blk, -offset, outer * inner))
    stock = jnp.stack(arrived, 0)
    slot_ids = (block_lists - (position - REACH)).astype(jnp.int32)
    attended, query_grad, running = attention(
        queries, out_grad, stock, slot_ids, list_counts.astype(jnp.int32)
    )
    owned = running[REACH]
    for offset in range(-REACH, REACH + 1):
        if offset != 0:
            sent = running[REACH + offset].astype(jnp.bfloat16)
            owned = owned + passed_along(sent, blk, offset, outer * inner).astype(jnp.float32)
    rounded = owned.astype(jnp.bfloat16)
    contract_cols = (((1,), (1,)), ((), ()))
    encoder_terms = lax.dot_general(
        rounded[0], key_weight, contract_cols, preferred_element_type=jnp.float32
    ) + lax.dot_general(rounded[1], value_weight, contract_cols, preferred_element_type=jnp.float32)
    encoder_grad = lax.psum_scatter(encoder_terms, "grp", scatter_dimension=1, tiled=True).astype(
        jnp.bfloat16
    )
    both_grads = jnp.concatenate([rounded[0], rounded[1]], 1)
    group_grads = lax.all_gather(both_grads, "byx", axis=0, tiled=True)
    rows = encoder.shape[0]
    slice_rows = model // (outer * inner)
    picked = lax.dynamic_slice_in_dim(
        near.reshape(inner * rows, outer, inner, slice_rows),
        lax.axis_index("byx"),
        1,
        axis=2,
    ).reshape(inner * rows, outer * slice_rows)
    partial = lax.dot_general(
        picked, group_grads, (((0,), (0,)), ((), ())), preferred_element_type=jnp.float32
    )
    weight_rows = lax.psum_scatter(partial, "bz", scatter_dimension=0, tiled=True)
    return (
        attended,
        query_grad,
        encoder_grad,
        weight_rows[:, :head_cols],
        weight_rows[:, head_cols:],
    )


def solution(mesh):
    blk_size, grp_size = mesh.devices.shape
    outer = 4 if blk_size % 4 == 0 else 1
    inner = blk_size // outer
    split = jax.sharding.Mesh(
        mesh.devices.reshape(outer, inner, grp_size), ("bz", "byx", "grp")
    )
    blk = ("bz", "byx")
    in_specs = (
        P(blk, "grp"),
        P(blk, None),
        P(None, "grp"),
        P(None, "grp"),
        P(blk, "grp"),
        P(blk, None),
        P(blk),
    )
    out_specs = (
        P(blk, "grp"),
        P(blk, "grp"),
        P(blk, "grp"),
        P(blk, "grp"),
        P(blk, "grp"),
    )
    return jax.shard_map(
        functools.partial(on_device, outer=outer, inner=inner),
        mesh=split,
        in_specs=in_specs,
        out_specs=out_specs,
        check_vma=False,
    )
```

```python
import functools

import jax
import jax.numpy as jnp
from jax import lax
from jax.experimental import pallas as pl
from jax.experimental.pallas import tpu as pltpu
from jax.sharding import PartitionSpec as P

HEAD_DIM = 64
REACH = 4
LISTED = 5
LANES = 128


def passed_along(value, axis, by, size):
    pairs = [(i, i + by) for i in range(size) if 0 <= i + by < size]
    return lax.ppermute(value, axis, pairs)


def attention_kernel(
    slots_ref, counts_ref, q_ref, g_ref, stock_ref, flipped_ref, out_ref, dq_ref, own_ref,
    sent_ref, acc_ref,
):
    factor = HEAD_DIM ** (-0.5)
    step = pl.program_id(0)

    @pl.when(step == 0)
    def _():
        acc_ref[...] = jnp.zeros_like(acc_ref)

    count = counts_ref[step]
    rows = q_ref.shape[0]
    lane = lax.broadcasted_iota(jnp.int32, (rows, LANES), 1)
    first = lane < HEAD_DIM
    row = lax.broadcasted_iota(jnp.int32, (LANES, rows), 0)
    top = row < HEAD_DIM
    slots = [slots_ref[step, j] for j in range(LISTED)]
    f32 = jnp.float32
    bf16 = jnp.bfloat16

    def dot(a, b):
        return jnp.dot(a, b, preferred_element_type=f32)

    def run(used):
        def pair(p, carry):
            off = pl.multiple_of(p * LANES, LANES)
            qp = q_ref[:, pl.ds(off, LANES)]
            gp = g_ref[:, pl.ds(off, LANES)]
            qt = qp.astype(f32).T * factor
            gt = gp.astype(f32).T * factor
            zf = jnp.zeros_like(qt)
            qst = [jnp.where(top, qt, zf).astype(bf16), jnp.where(top, zf, qt).astype(bf16)]
            gst = [jnp.where(top, gt, zf).astype(bf16), jnp.where(top, zf, gt).astype(bf16)]
            zq = jnp.zeros_like(qp)
            qh = [jnp.where(first, qp, zq), jnp.where(first, zq, qp)]
            gh = [jnp.where(first, gp, zq), jnp.where(first, zq, gp)]
            ks = [stock_ref[slots[j], 0, :, pl.ds(off, LANES)] for j in range(used)]
            vs = [stock_ref[slots[j], 1, :, pl.ds(off, LANES)] for j in range(used)]
            kts = [flipped_ref[slots[j], 0, pl.ds(off, LANES), :] for j in range(used)]
            vts = [flipped_ref[slots[j], 1, pl.ds(off, LANES), :] for j in range(used)]
            outs, dqs = [], []
            dks = [None] * used
            dvs = [None] * used
            for h in range(2):
                scores = [dot(ks[j], qst[h]) for j in range(used)]
                peak = jnp.max(scores[0], axis=0, keepdims=True)
                for j in range(1, used):
                    peak = jnp.maximum(peak, jnp.max(scores[j], axis=0, keepdims=True))
                expos = [jnp.exp(sc - peak) for sc in scores]
                total = jnp.sum(expos[0], axis=0, keepdims=True)
                for j in range(1, used):
                    total = total + jnp.sum(expos[j], axis=0, keepdims=True)
                inverse = 1.0 / total
                ws = [(e * inverse).astype(bf16) for e in expos]
                out = dot(vts[0], ws[0])
                for j in range(1, used):
                    out = out + dot(vts[j], ws[j])
                dws = [dot(vs[j], gst[h]) for j in range(used)]
                wf = [w.astype(f32) for w in ws]
                center = jnp.sum(wf[0] * dws[0], axis=0, keepdims=True)
                for j in range(1, used):
                    center = center + jnp.sum(wf[j] * dws[j], axis=0, keepdims=True)
                dss = [(wf[j] * (dws[j] - center)).astype(bf16) for j in range(used)]
                dq = dot(kts[0], dss[0])
                for j in range(1, used):
                    dq = dq + dot(kts[j], dss[j])
                for j in range(used):
                    dk = dot(dss[j], qh[h])
                    dv = dot(ws[j], gh[h])
                    dks[j] = dk if dks[j] is None else dks[j] + dk
                    dvs[j] = dv if dvs[j] is None else dvs[j] + dv
                outs.append(out)
                dqs.append(dq)
            out_ref[:, pl.ds(off, LANES)] = jnp.where(top, outs[0], outs[1]).T.astype(out_ref.dtype)
            dq_ref[:, pl.ds(off, LANES)] = jnp.where(top, dqs[0], dqs[1]).T.astype(dq_ref.dtype)
            for j in range(used):
                acc_ref[slots[j], 0, :, pl.ds(off, LANES)] += dks[j]
                acc_ref[slots[j], 1, :, pl.ds(off, LANES)] += dvs[j]
            return carry

        lax.fori_loop(0, q_ref.shape[1] // LANES, pair, 0, unroll=True)

    for used in range(1, LISTED + 1):
        pl.when(count == used)(functools.partial(run, used))

    @pl.when(step == pl.num_programs(0) - 1)
    def _():
        own_ref[...] = acc_ref[REACH]
        sent_ref[...] = acc_ref[...].astype(sent_ref.dtype)


def attention(queries, out_grad, stock, slot_ids, counts):
    rows, cols = stock.shape[2], stock.shape[3]
    blocks = queries.shape[0] // rows
    n_slots = stock.shape[0]
    flipped = jnp.swapaxes(stock, 2, 3)
    flops = blocks * (cols // LANES) * 2 * 3 * 6 * 2 * rows * LANES * LANES
    bytes_accessed = 4 * queries.size * 2 + 2 * stock.size * 2 + stock.size * 4
    grid_spec = pltpu.PrefetchScalarGridSpec(
        num_scalar_prefetch=2,
        grid=(blocks,),
        in_specs=[
            pl.BlockSpec((rows, cols), lambda i, s, c: (i, 0)),
            pl.BlockSpec((rows, cols), lambda i, s, c: (i, 0)),
            pl.BlockSpec((n_slots, 2, rows, cols), lambda i, s, c: (0, 0, 0, 0)),
            pl.BlockSpec((n_slots, 2, cols, rows), lambda i, s, c: (0, 0, 0, 0)),
        ],
        out_specs=[
            pl.BlockSpec((rows, cols), lambda i, s, c: (i, 0)),
            pl.BlockSpec((rows, cols), lambda i, s, c: (i, 0)),
            pl.BlockSpec((2, rows, cols), lambda i, s, c: (0, 0, 0)),
            pl.BlockSpec((n_slots, 2, rows, cols), lambda i, s, c: (0, 0, 0, 0)),
        ],
        scratch_shapes=[pltpu.VMEM(stock.shape, jnp.float32)],
    )
    return pl.pallas_call(
        attention_kernel,
        grid_spec=grid_spec,
        out_shape=[
            jax.ShapeDtypeStruct(queries.shape, jnp.bfloat16),
            jax.ShapeDtypeStruct(queries.shape, jnp.bfloat16),
            jax.ShapeDtypeStruct(stock.shape[1:], jnp.float32),
            jax.ShapeDtypeStruct(stock.shape, jnp.bfloat16),
        ],
        compiler_params=pltpu.CompilerParams(dimension_semantics=("arbitrary",)),
        cost_estimate=pl.CostEstimate(
            flops=flops, transcendentals=blocks * rows * 3 * rows * (cols // HEAD_DIM),
            bytes_accessed=bytes_accessed,
        ),
    )(slot_ids, counts, queries, out_grad, stock, flipped)


def on_device(
    queries, encoder, key_weight, value_weight, out_grad, block_lists, list_counts, outer, inner
):
    blk = ("bz", "byx")
    position = lax.axis_index(blk)
    head_cols = key_weight.shape[1]
    model = encoder.shape[1]
    near = lax.all_gather(encoder, "byx", axis=0, tiled=False)
    own_keys = jnp.dot(encoder, key_weight, preferred_element_type=jnp.float32).astype(jnp.bfloat16)
    own_values = jnp.dot(encoder, value_weight, preferred_element_type=jnp.float32).astype(
        jnp.bfloat16
    )
    own = jnp.stack([own_keys, own_values], 0)
    arrived = []
    for offset in range(-REACH, REACH + 1):
        if offset == 0:
            arrived.append(own)
        else:
            arrived.append(passed_along(own, blk, -offset, outer * inner))
    stock = jnp.stack(arrived, 0)
    slot_ids = (block_lists - (position - REACH)).astype(jnp.int32)
    attended, query_grad, owned, sending = attention(
        queries, out_grad, stock, slot_ids, list_counts.astype(jnp.int32)
    )
    for offset in range(-REACH, REACH + 1):
        if offset != 0:
            sent = sending[REACH + offset]
            owned = owned + passed_along(sent, blk, offset, outer * inner).astype(jnp.float32)
    rounded = owned.astype(jnp.bfloat16)
    contract_cols = (((1,), (1,)), ((), ()))
    encoder_terms = lax.dot_general(
        rounded[0], key_weight, contract_cols, preferred_element_type=jnp.float32
    ) + lax.dot_general(rounded[1], value_weight, contract_cols, preferred_element_type=jnp.float32)
    encoder_grad = lax.psum_scatter(encoder_terms, "grp", scatter_dimension=1, tiled=True).astype(
        jnp.bfloat16
    )
    both_grads = jnp.concatenate([rounded[0], rounded[1]], 1)
    group_grads = lax.all_gather(both_grads, "byx", axis=0, tiled=True)
    rows = encoder.shape[0]
    slice_rows = model // (outer * inner)
    picked = lax.dynamic_slice_in_dim(
        near.reshape(inner * rows, outer, inner, slice_rows),
        lax.axis_index("byx"),
        1,
        axis=2,
    ).reshape(inner * rows, outer * slice_rows)
    partial = lax.dot_general(
        picked, group_grads, (((0,), (0,)), ((), ())), preferred_element_type=jnp.float32
    )
    weight_rows = lax.psum_scatter(partial, "bz", scatter_dimension=0, tiled=True)
    return (
        attended,
        query_grad,
        encoder_grad,
        weight_rows[:, :head_cols],
        weight_rows[:, head_cols:],
    )


def solution(mesh):
    blk_size, grp_size = mesh.devices.shape
    outer = 4 if blk_size % 4 == 0 else 1
    inner = blk_size // outer
    split = jax.sharding.Mesh(
        mesh.devices.reshape(outer, inner, grp_size), ("bz", "byx", "grp")
    )
    blk = ("bz", "byx")
    in_specs = (
        P(blk, "grp"),
        P(blk, None),
        P(None, "grp"),
        P(None, "grp"),
        P(blk, "grp"),
        P(blk, None),
        P(blk),
    )
    out_specs = (
        P(blk, "grp"),
        P(blk, "grp"),
        P(blk, "grp"),
        P(blk, "grp"),
        P(blk, "grp"),
    )
    return jax.shard_map(
        functools.partial(on_device, outer=outer, inner=inner),
        mesh=split,
        in_specs=in_specs,
        out_specs=out_specs,
        check_vma=False,
    )
```

```python
import functools

import jax
import jax.numpy as jnp
from jax import lax
from jax.experimental import pallas as pl
from jax.experimental.pallas import tpu as pltpu
from jax.sharding import PartitionSpec as P

HEAD_DIM = 64
REACH = 4
LISTED = 5
LANES = 128


def passed_along(value, axis, by, size):
    pairs = [(i, i + by) for i in range(size) if 0 <= i + by < size]
    return lax.ppermute(value, axis, pairs)


def attention_kernel(
    slots_ref, counts_ref, q_ref, g_ref, stock_ref, flipped_ref, out_ref, dq_ref, own_ref,
    sent_ref, acc_ref,
):
    factor = HEAD_DIM ** (-0.5)
    step = pl.program_id(0)

    @pl.when(step == 0)
    def _():
        acc_ref[...] = jnp.zeros_like(acc_ref)

    count = counts_ref[step]
    rows = q_ref.shape[0]
    lane = lax.broadcasted_iota(jnp.int32, (rows, LANES), 1)
    first = lane < HEAD_DIM
    row = lax.broadcasted_iota(jnp.int32, (LANES, rows), 0)
    top = row < HEAD_DIM
    slots = [slots_ref[step, j] for j in range(LISTED)]
    f32 = jnp.float32
    bf16 = jnp.bfloat16

    def dot(a, b):
        return jnp.dot(a, b, preferred_element_type=f32)

    def run(used):
        def pair(p, carry):
            off = pl.multiple_of(p * LANES, LANES)
            qp = q_ref[:, pl.ds(off, LANES)]
            gp = g_ref[:, pl.ds(off, LANES)]
            qt = qp.astype(f32).T * factor
            gt = gp.astype(f32).T * factor
            zf = jnp.zeros_like(qt)
            qst = [jnp.where(top, qt, zf).astype(bf16), jnp.where(top, zf, qt).astype(bf16)]
            gst = [jnp.where(top, gt, zf).astype(bf16), jnp.where(top, zf, gt).astype(bf16)]
            zq = jnp.zeros_like(qp)
            qh = [jnp.where(first, qp, zq), jnp.where(first, zq, qp)]
            gh = [jnp.where(first, gp, zq), jnp.where(first, zq, gp)]
            ks = [stock_ref[slots[j], 0, :, pl.ds(off, LANES)] for j in range(used)]
            vs = [stock_ref[slots[j], 1, :, pl.ds(off, LANES)] for j in range(used)]
            kts = [flipped_ref[slots[j], 0, pl.ds(off, LANES), :] for j in range(used)]
            vts = [flipped_ref[slots[j], 1, pl.ds(off, LANES), :] for j in range(used)]
            outs, dqs = [], []
            dks = [None] * used
            dvs = [None] * used
            for h in range(2):
                scores = [dot(ks[j], qst[h]) for j in range(used)]
                peak = jnp.max(scores[0], axis=0, keepdims=True)
                for j in range(1, used):
                    peak = jnp.maximum(peak, jnp.max(scores[j], axis=0, keepdims=True))
                expos = [jnp.exp(sc - peak) for sc in scores]
                total = jnp.sum(expos[0], axis=0, keepdims=True)
                for j in range(1, used):
                    total = total + jnp.sum(expos[j], axis=0, keepdims=True)
                inverse = 1.0 / total
                ws = [(e * inverse).astype(bf16) for e in expos]
                out = dot(vts[0], ws[0])
                for j in range(1, used):
                    out = out + dot(vts[j], ws[j])
                dws = [dot(vs[j], gst[h]) for j in range(used)]
                wf = [w.astype(f32) for w in ws]
                center = jnp.sum(wf[0] * dws[0], axis=0, keepdims=True)
                for j in range(1, used):
                    center = center + jnp.sum(wf[j] * dws[j], axis=0, keepdims=True)
                dss = [(wf[j] * (dws[j] - center)).astype(bf16) for j in range(used)]
                dq = dot(kts[0], dss[0])
                for j in range(1, used):
                    dq = dq + dot(kts[j], dss[j])
                for j in range(used):
                    dk = dot(dss[j], qh[h])
                    dv = dot(ws[j], gh[h])
                    dks[j] = dk if dks[j] is None else dks[j] + dk
                    dvs[j] = dv if dvs[j] is None else dvs[j] + dv
                outs.append(out)
                dqs.append(dq)
            out_ref[:, pl.ds(off, LANES)] = jnp.where(top, outs[0], outs[1]).T.astype(out_ref.dtype)
            dq_ref[:, pl.ds(off, LANES)] = jnp.where(top, dqs[0], dqs[1]).T.astype(dq_ref.dtype)
            for j in range(used):
                acc_ref[slots[j], 0, :, pl.ds(off, LANES)] += dks[j]
                acc_ref[slots[j], 1, :, pl.ds(off, LANES)] += dvs[j]
            return carry

        lax.fori_loop(0, q_ref.shape[1] // LANES, pair, 0, unroll=True)

    for used in range(1, LISTED + 1):
        pl.when(count == used)(functools.partial(run, used))

    @pl.when(step == pl.num_programs(0) - 1)
    def _():
        own_ref[...] = acc_ref[REACH]
        sent_ref[...] = acc_ref[...].astype(sent_ref.dtype)


def attention(queries, out_grad, stock, slot_ids, counts):
    rows, cols = stock.shape[2], stock.shape[3]
    blocks = queries.shape[0] // rows
    n_slots = stock.shape[0]
    flipped = jnp.swapaxes(stock, 2, 3)
    flops = blocks * (cols // LANES) * 2 * 3 * 6 * 2 * rows * LANES * LANES
    bytes_accessed = 4 * queries.size * 2 + 2 * stock.size * 2 + stock.size * 4
    grid_spec = pltpu.PrefetchScalarGridSpec(
        num_scalar_prefetch=2,
        grid=(blocks,),
        in_specs=[
            pl.BlockSpec((rows, cols), lambda i, s, c: (i, 0)),
            pl.BlockSpec((rows, cols), lambda i, s, c: (i, 0)),
            pl.BlockSpec((n_slots, 2, rows, cols), lambda i, s, c: (0, 0, 0, 0)),
            pl.BlockSpec((n_slots, 2, cols, rows), lambda i, s, c: (0, 0, 0, 0)),
        ],
        out_specs=[
            pl.BlockSpec((rows, cols), lambda i, s, c: (i, 0)),
            pl.BlockSpec((rows, cols), lambda i, s, c: (i, 0)),
            pl.BlockSpec((2, rows, cols), lambda i, s, c: (0, 0, 0)),
            pl.BlockSpec((n_slots, 2, rows, cols), lambda i, s, c: (0, 0, 0, 0)),
        ],
        scratch_shapes=[pltpu.VMEM(stock.shape, jnp.float32)],
    )
    return pl.pallas_call(
        attention_kernel,
        grid_spec=grid_spec,
        out_shape=[
            jax.ShapeDtypeStruct(queries.shape, jnp.bfloat16),
            jax.ShapeDtypeStruct(queries.shape, jnp.bfloat16),
            jax.ShapeDtypeStruct(stock.shape[1:], jnp.float32),
            jax.ShapeDtypeStruct(stock.shape, jnp.bfloat16),
        ],
        compiler_params=pltpu.CompilerParams(dimension_semantics=("arbitrary",)),
        cost_estimate=pl.CostEstimate(
            flops=flops, transcendentals=blocks * rows * 3 * rows * (cols // HEAD_DIM),
            bytes_accessed=bytes_accessed,
        ),
    )(slot_ids, counts, queries, out_grad, stock, flipped)


def on_device(
    queries, encoder, key_weight, value_weight, out_grad, block_lists, list_counts, outer, inner
):
    blk = ("bz", "byx")
    position = lax.axis_index(blk)
    head_cols = key_weight.shape[1]
    model = encoder.shape[1]
    near = lax.all_gather(encoder, "byx", axis=0, tiled=False)
    own_keys = jnp.dot(encoder, key_weight, preferred_element_type=jnp.float32).astype(jnp.bfloat16)
    own_values = jnp.dot(encoder, value_weight, preferred_element_type=jnp.float32).astype(
        jnp.bfloat16
    )
    own = jnp.stack([own_keys, own_values], 0)
    arrived = []
    for offset in range(-REACH, REACH + 1):
        if offset == 0:
            arrived.append(own)
        else:
            arrived.append(passed_along(own, blk, -offset, outer * inner))
    stock = jnp.stack(arrived, 0)
    slot_ids = (block_lists - (position - REACH)).astype(jnp.int32)
    attended, query_grad, owned, sending = attention(
        queries, out_grad, stock, slot_ids, list_counts.astype(jnp.int32)
    )
    for offset in range(-REACH, REACH + 1):
        if offset != 0:
            sent = sending[REACH + offset]
            owned = owned + passed_along(sent, blk, offset, outer * inner).astype(jnp.float32)
    rounded = owned.astype(jnp.bfloat16)
    contract_cols = (((1,), (1,)), ((), ()))
    encoder_terms = lax.dot_general(
        rounded[0], key_weight, contract_cols, preferred_element_type=jnp.float32
    ) + lax.dot_general(rounded[1], value_weight, contract_cols, preferred_element_type=jnp.float32)
    encoder_grad = lax.psum_scatter(encoder_terms, "grp", scatter_dimension=1, tiled=True).astype(
        jnp.bfloat16
    )
    group_keys = lax.all_gather(rounded[0], "byx", axis=0, tiled=True)
    group_values = lax.all_gather(rounded[1], "byx", axis=0, tiled=True)
    rows = encoder.shape[0]
    slice_rows = model // (outer * inner)
    picked = lax.dynamic_slice_in_dim(
        near.reshape(inner * rows, outer, inner, slice_rows),
        lax.axis_index("byx"),
        1,
        axis=2,
    ).reshape(inner * rows, outer * slice_rows)
    contract_rows = (((0,), (0,)), ((), ()))
    partial = jnp.concatenate(
        [
            lax.dot_general(picked, group_keys, contract_rows, preferred_element_type=jnp.float32),
            lax.dot_general(picked, group_values, contract_rows, preferred_element_type=jnp.float32),
        ],
        1,
    )
    weight_rows = lax.psum_scatter(partial, "bz", scatter_dimension=0, tiled=True)
    return (
        attended,
        query_grad,
        encoder_grad,
        weight_rows[:, :head_cols],
        weight_rows[:, head_cols:],
    )


def solution(mesh):
    blk_size, grp_size = mesh.devices.shape
    outer = 4 if blk_size % 4 == 0 else 1
    inner = blk_size // outer
    split = jax.sharding.Mesh(
        mesh.devices.reshape(outer, inner, grp_size), ("bz", "byx", "grp")
    )
    blk = ("bz", "byx")
    in_specs = (
        P(blk, "grp"),
        P(blk, None),
        P(None, "grp"),
        P(None, "grp"),
        P(blk, "grp"),
        P(blk, None),
        P(blk),
    )
    out_specs = (
        P(blk, "grp"),
        P(blk, "grp"),
        P(blk, "grp"),
        P(blk, "grp"),
        P(blk, "grp"),
    )
    return jax.shard_map(
        functools.partial(on_device, outer=outer, inner=inner),
        mesh=split,
        in_specs=in_specs,
        out_specs=out_specs,
        check_vma=False,
    )
```

```python
import functools

import jax
import jax.numpy as jnp
from jax import lax
from jax.experimental import pallas as pl
from jax.experimental.pallas import tpu as pltpu
from jax.sharding import PartitionSpec as P

HEAD_DIM = 64
REACH = 4
LISTED = 5
LANES = 128


def passed_along(value, axis, by, size):
    pairs = [(i, i + by) for i in range(size) if 0 <= i + by < size]
    return lax.ppermute(value, axis, pairs)


def attention_kernel(
    slots_ref, counts_ref, q_ref, g_ref, stock_ref, out_ref, dq_ref, own_ref,
    sent_ref, acc_ref, flipped_ref,
):
    factor = HEAD_DIM ** (-0.5)
    step = pl.program_id(0)

    @pl.when(step == 0)
    def _():
        acc_ref[...] = jnp.zeros_like(acc_ref)

        def flip(s, carry):
            for kind in range(2):
                for p in range(stock_ref.shape[3] // LANES):
                    piece = stock_ref[s, kind, :, pl.ds(p * LANES, LANES)]
                    flipped_ref[s, kind, pl.ds(p * LANES, LANES), :] = (
                        piece.astype(jnp.float32).T.astype(flipped_ref.dtype)
                    )
            return carry

        lax.fori_loop(0, stock_ref.shape[0], flip, 0)

    count = counts_ref[step]
    rows = q_ref.shape[0]
    lane = lax.broadcasted_iota(jnp.int32, (rows, LANES), 1)
    first = lane < HEAD_DIM
    row = lax.broadcasted_iota(jnp.int32, (LANES, rows), 0)
    top = row < HEAD_DIM
    slots = [slots_ref[step, j] for j in range(LISTED)]
    f32 = jnp.float32
    bf16 = jnp.bfloat16

    def dot(a, b):
        return jnp.dot(a, b, preferred_element_type=f32)

    def run(used):
        def pair(p, carry):
            off = pl.multiple_of(p * LANES, LANES)
            qp = q_ref[:, pl.ds(off, LANES)]
            gp = g_ref[:, pl.ds(off, LANES)]
            qt = qp.astype(f32).T * factor
            gt = gp.astype(f32).T * factor
            zf = jnp.zeros_like(qt)
            qst = [jnp.where(top, qt, zf).astype(bf16), jnp.where(top, zf, qt).astype(bf16)]
            gst = [jnp.where(top, gt, zf).astype(bf16), jnp.where(top, zf, gt).astype(bf16)]
            zq = jnp.zeros_like(qp)
            qh = [jnp.where(first, qp, zq), jnp.where(first, zq, qp)]
            gh = [jnp.where(first, gp, zq), jnp.where(first, zq, gp)]
            ks = [stock_ref[slots[j], 0, :, pl.ds(off, LANES)] for j in range(used)]
            vs = [stock_ref[slots[j], 1, :, pl.ds(off, LANES)] for j in range(used)]
            kts = [flipped_ref[slots[j], 0, pl.ds(off, LANES), :] for j in range(used)]
            vts = [flipped_ref[slots[j], 1, pl.ds(off, LANES), :] for j in range(used)]
            outs, dqs = [], []
            dks = [None] * used
            dvs = [None] * used
            for h in range(2):
                scores = [dot(ks[j], qst[h]) for j in range(used)]
                peak = jnp.max(scores[0], axis=0, keepdims=True)
                for j in range(1, used):
                    peak = jnp.maximum(peak, jnp.max(scores[j], axis=0, keepdims=True))
                expos = [jnp.exp(sc - peak) for sc in scores]
                total = jnp.sum(expos[0], axis=0, keepdims=True)
                for j in range(1, used):
                    total = total + jnp.sum(expos[j], axis=0, keepdims=True)
                inverse = 1.0 / total
                ws = [(e * inverse).astype(bf16) for e in expos]
                out = dot(vts[0], ws[0])
                for j in range(1, used):
                    out = out + dot(vts[j], ws[j])
                dws = [dot(vs[j], gst[h]) for j in range(used)]
                wf = [w.astype(f32) for w in ws]
                center = jnp.sum(wf[0] * dws[0], axis=0, keepdims=True)
                for j in range(1, used):
                    center = center + jnp.sum(wf[j] * dws[j], axis=0, keepdims=True)
                dss = [(wf[j] * (dws[j] - center)).astype(bf16) for j in range(used)]
                dq = dot(kts[0], dss[0])
                for j in range(1, used):
                    dq = dq + dot(kts[j], dss[j])
                for j in range(used):
                    dk = dot(dss[j], qh[h])
                    dv = dot(ws[j], gh[h])
                    dks[j] = dk if dks[j] is None else dks[j] + dk
                    dvs[j] = dv if dvs[j] is None else dvs[j] + dv
                outs.append(out)
                dqs.append(dq)
            out_ref[:, pl.ds(off, LANES)] = jnp.where(top, outs[0], outs[1]).T.astype(out_ref.dtype)
            dq_ref[:, pl.ds(off, LANES)] = jnp.where(top, dqs[0], dqs[1]).T.astype(dq_ref.dtype)
            for j in range(used):
                acc_ref[slots[j], 0, :, pl.ds(off, LANES)] += dks[j]
                acc_ref[slots[j], 1, :, pl.ds(off, LANES)] += dvs[j]
            return carry

        lax.fori_loop(0, q_ref.shape[1] // LANES, pair, 0, unroll=True)

    for used in range(1, LISTED + 1):
        pl.when(count == used)(functools.partial(run, used))

    @pl.when(step == pl.num_programs(0) - 1)
    def _():
        own_ref[...] = acc_ref[REACH]
        sent_ref[...] = acc_ref[...].astype(sent_ref.dtype)


def attention(queries, out_grad, stock, slot_ids, counts):
    rows, cols = stock.shape[2], stock.shape[3]
    blocks = queries.shape[0] // rows
    n_slots = stock.shape[0]
    flops = blocks * (cols // LANES) * 2 * 3 * 6 * 2 * rows * LANES * LANES
    bytes_accessed = 4 * queries.size * 2 + stock.size * 2 + stock.size * 4
    grid_spec = pltpu.PrefetchScalarGridSpec(
        num_scalar_prefetch=2,
        grid=(blocks,),
        in_specs=[
            pl.BlockSpec((rows, cols), lambda i, s, c: (i, 0)),
            pl.BlockSpec((rows, cols), lambda i, s, c: (i, 0)),
            pl.BlockSpec((n_slots, 2, rows, cols), lambda i, s, c: (0, 0, 0, 0)),
        ],
        out_specs=[
            pl.BlockSpec((rows, cols), lambda i, s, c: (i, 0)),
            pl.BlockSpec((rows, cols), lambda i, s, c: (i, 0)),
            pl.BlockSpec((2, rows, cols), lambda i, s, c: (0, 0, 0)),
            pl.BlockSpec((n_slots, 2, rows, cols), lambda i, s, c: (0, 0, 0, 0)),
        ],
        scratch_shapes=[
            pltpu.VMEM(stock.shape, jnp.float32),
            pltpu.VMEM((n_slots, 2, cols, rows), stock.dtype),
        ],
    )
    return pl.pallas_call(
        attention_kernel,
        grid_spec=grid_spec,
        out_shape=[
            jax.ShapeDtypeStruct(queries.shape, jnp.bfloat16),
            jax.ShapeDtypeStruct(queries.shape, jnp.bfloat16),
            jax.ShapeDtypeStruct(stock.shape[1:], jnp.float32),
            jax.ShapeDtypeStruct(stock.shape, jnp.bfloat16),
        ],
        compiler_params=pltpu.CompilerParams(dimension_semantics=("arbitrary",)),
        cost_estimate=pl.CostEstimate(
            flops=flops, transcendentals=blocks * rows * 3 * rows * (cols // HEAD_DIM),
            bytes_accessed=bytes_accessed,
        ),
    )(slot_ids, counts, queries, out_grad, stock)


def on_device(
    queries, encoder, key_weight, value_weight, out_grad, block_lists, list_counts, outer, inner
):
    blk = ("bz", "byx")
    position = lax.axis_index(blk)
    head_cols = key_weight.shape[1]
    model = encoder.shape[1]
    near = lax.all_gather(encoder, "byx", axis=0, tiled=False)
    own_keys = jnp.dot(encoder, key_weight, preferred_element_type=jnp.float32).astype(jnp.bfloat16)
    own_values = jnp.dot(encoder, value_weight, preferred_element_type=jnp.float32).astype(
        jnp.bfloat16
    )
    own = jnp.stack([own_keys, own_values], 0)
    arrived = []
    for offset in range(-REACH, REACH + 1):
        if offset == 0:
            arrived.append(own)
        else:
            arrived.append(passed_along(own, blk, -offset, outer * inner))
    stock = jnp.stack(arrived, 0)
    slot_ids = (block_lists - (position - REACH)).astype(jnp.int32)
    attended, query_grad, owned, sending = attention(
        queries, out_grad, stock, slot_ids, list_counts.astype(jnp.int32)
    )
    for offset in range(-REACH, REACH + 1):
        if offset != 0:
            sent = sending[REACH + offset]
            owned = owned + passed_along(sent, blk, offset, outer * inner).astype(jnp.float32)
    rounded = owned.astype(jnp.bfloat16)
    contract_cols = (((1,), (1,)), ((), ()))
    encoder_terms = lax.dot_general(
        rounded[0], key_weight, contract_cols, preferred_element_type=jnp.float32
    ) + lax.dot_general(rounded[1], value_weight, contract_cols, preferred_element_type=jnp.float32)
    encoder_grad = lax.psum_scatter(encoder_terms, "grp", scatter_dimension=1, tiled=True).astype(
        jnp.bfloat16
    )
    both_grads = jnp.concatenate([rounded[0], rounded[1]], 1)
    group_grads = lax.all_gather(both_grads, "byx", axis=0, tiled=True)
    rows = encoder.shape[0]
    slice_rows = model // (outer * inner)
    picked = lax.dynamic_slice_in_dim(
        near.reshape(inner * rows, outer, inner, slice_rows),
        lax.axis_index("byx"),
        1,
        axis=2,
    ).reshape(inner * rows, outer * slice_rows)
    partial = lax.dot_general(
        picked, group_grads, (((0,), (0,)), ((), ())), preferred_element_type=jnp.float32
    )
    weight_rows = lax.psum_scatter(partial, "bz", scatter_dimension=0, tiled=True)
    return (
        attended,
        query_grad,
        encoder_grad,
        weight_rows[:, :head_cols],
        weight_rows[:, head_cols:],
    )


def solution(mesh):
    blk_size, grp_size = mesh.devices.shape
    outer = 4 if blk_size % 4 == 0 else 1
    inner = blk_size // outer
    split = jax.sharding.Mesh(
        mesh.devices.reshape(outer, inner, grp_size), ("bz", "byx", "grp")
    )
    blk = ("bz", "byx")
    in_specs = (
        P(blk, "grp"),
        P(blk, None),
        P(None, "grp"),
        P(None, "grp"),
        P(blk, "grp"),
        P(blk, None),
        P(blk),
    )
    out_specs = (
        P(blk, "grp"),
        P(blk, "grp"),
        P(blk, "grp"),
        P(blk, "grp"),
        P(blk, "grp"),
    )
    return jax.shard_map(
        functools.partial(on_device, outer=outer, inner=inner),
        mesh=split,
        in_specs=in_specs,
        out_specs=out_specs,
        check_vma=False,
    )
```

```python
import functools

import jax
import jax.numpy as jnp
from jax import lax
from jax.experimental import pallas as pl
from jax.experimental.pallas import tpu as pltpu
from jax.sharding import PartitionSpec as P

HEAD_DIM = 64
REACH = 4
LISTED = 5
LANES = 128


def passed_along(value, axis, by, size):
    pairs = [(i, i + by) for i in range(size) if 0 <= i + by < size]
    return lax.ppermute(value, axis, pairs)


def attention_kernel(
    slots_ref, counts_ref, q_ref, g_ref, stock_ref, out_ref, dq_ref, own_ref,
    sent_ref, acc_ref, flipped_ref,
):
    factor = HEAD_DIM ** (-0.5)
    step = pl.program_id(0)

    @pl.when(step == 0)
    def _():
        acc_ref[...] = jnp.zeros_like(acc_ref)

        def flip(s, carry):
            for kind in range(2):
                for p in range(stock_ref.shape[3] // LANES):
                    piece = stock_ref[s, kind, :, pl.ds(p * LANES, LANES)]
                    flipped_ref[s, kind, pl.ds(p * LANES, LANES), :] = (
                        piece.astype(jnp.float32).T.astype(flipped_ref.dtype)
                    )
            return carry

        lax.fori_loop(0, stock_ref.shape[0], flip, 0)

    count = counts_ref[step]
    rows = q_ref.shape[0]
    lane = lax.broadcasted_iota(jnp.int32, (rows, LANES), 1)
    first = lane < HEAD_DIM
    row = lax.broadcasted_iota(jnp.int32, (LANES, rows), 0)
    top = row < HEAD_DIM
    slots = [slots_ref[step, j] for j in range(LISTED)]
    f32 = jnp.float32
    bf16 = jnp.bfloat16

    def dot(a, b):
        return jnp.dot(a, b, preferred_element_type=f32)

    def run(used):
        def pair(p, carry):
            off = pl.multiple_of(p * LANES, LANES)
            qp = q_ref[:, pl.ds(off, LANES)]
            gp = g_ref[:, pl.ds(off, LANES)]
            qt = qp.astype(f32).T * factor
            gt = gp.astype(f32).T * factor
            zf = jnp.zeros_like(qt)
            qst = [jnp.where(top, qt, zf).astype(bf16), jnp.where(top, zf, qt).astype(bf16)]
            gst = [jnp.where(top, gt, zf).astype(bf16), jnp.where(top, zf, gt).astype(bf16)]
            zq = jnp.zeros_like(qp)
            qh = [jnp.where(first, qp, zq), jnp.where(first, zq, qp)]
            gh = [jnp.where(first, gp, zq), jnp.where(first, zq, gp)]
            ks = [stock_ref[slots[j], 0, :, pl.ds(off, LANES)] for j in range(used)]
            vs = [stock_ref[slots[j], 1, :, pl.ds(off, LANES)] for j in range(used)]
            kts = [flipped_ref[slots[j], 0, pl.ds(off, LANES), :] for j in range(used)]
            vts = [flipped_ref[slots[j], 1, pl.ds(off, LANES), :] for j in range(used)]
            outs, dqs = [], []
            dks = [None] * used
            dvs = [None] * used
            for h in range(2):
                scores = [dot(ks[j], qst[h]) for j in range(used)]
                peak = jnp.max(scores[0], axis=0, keepdims=True)
                for j in range(1, used):
                    peak = jnp.maximum(peak, jnp.max(scores[j], axis=0, keepdims=True))
                expos = [jnp.exp(sc - peak) for sc in scores]
                total = jnp.sum(expos[0], axis=0, keepdims=True)
                for j in range(1, used):
                    total = total + jnp.sum(expos[j], axis=0, keepdims=True)
                inverse = 1.0 / total
                ws = [(e * inverse).astype(bf16) for e in expos]
                out = dot(vts[0], ws[0])
                for j in range(1, used):
                    out = out + dot(vts[j], ws[j])
                dws = [dot(vs[j], gst[h]) for j in range(used)]
                wf = [w.astype(f32) for w in ws]
                center = jnp.sum(wf[0] * dws[0], axis=0, keepdims=True)
                for j in range(1, used):
                    center = center + jnp.sum(wf[j] * dws[j], axis=0, keepdims=True)
                dss = [(wf[j] * (dws[j] - center)).astype(bf16) for j in range(used)]
                dq = dot(kts[0], dss[0])
                for j in range(1, used):
                    dq = dq + dot(kts[j], dss[j])
                for j in range(used):
                    dk = dot(dss[j], qh[h])
                    dv = dot(ws[j], gh[h])
                    dks[j] = dk if dks[j] is None else dks[j] + dk
                    dvs[j] = dv if dvs[j] is None else dvs[j] + dv
                outs.append(out)
                dqs.append(dq)
            out_ref[:, pl.ds(off, LANES)] = jnp.where(top, outs[0], outs[1]).T.astype(out_ref.dtype)
            dq_ref[:, pl.ds(off, LANES)] = jnp.where(top, dqs[0], dqs[1]).T.astype(dq_ref.dtype)
            for j in range(used):
                acc_ref[slots[j], 0, :, pl.ds(off, LANES)] += dks[j]
                acc_ref[slots[j], 1, :, pl.ds(off, LANES)] += dvs[j]
            return carry

        lax.fori_loop(0, q_ref.shape[1] // LANES, pair, 0, unroll=True)

    for used in range(1, LISTED + 1):
        pl.when(count == used)(functools.partial(run, used))

    @pl.when(step == pl.num_programs(0) - 1)
    def _():
        own_ref[...] = acc_ref[REACH]
        sent_ref[...] = acc_ref[...].astype(sent_ref.dtype)


def attention(queries, out_grad, stock, slot_ids, counts):
    rows, cols = stock.shape[2], stock.shape[3]
    blocks = queries.shape[0] // rows
    n_slots = stock.shape[0]
    flops = blocks * (cols // LANES) * 2 * 3 * 6 * 2 * rows * LANES * LANES
    bytes_accessed = 4 * queries.size * 2 + stock.size * 2 + stock.size * 4
    grid_spec = pltpu.PrefetchScalarGridSpec(
        num_scalar_prefetch=2,
        grid=(blocks,),
        in_specs=[
            pl.BlockSpec((rows, cols), lambda i, s, c: (i, 0)),
            pl.BlockSpec((rows, cols), lambda i, s, c: (i, 0)),
            pl.BlockSpec((n_slots, 2, rows, cols), lambda i, s, c: (0, 0, 0, 0)),
        ],
        out_specs=[
            pl.BlockSpec((rows, cols), lambda i, s, c: (i, 0)),
            pl.BlockSpec((rows, cols), lambda i, s, c: (i, 0)),
            pl.BlockSpec((2, rows, cols), lambda i, s, c: (0, 0, 0)),
            pl.BlockSpec((n_slots, 2, rows, cols), lambda i, s, c: (0, 0, 0, 0)),
        ],
        scratch_shapes=[
            pltpu.VMEM(stock.shape, jnp.float32),
            pltpu.VMEM((n_slots, 2, cols, rows), stock.dtype),
        ],
    )
    return pl.pallas_call(
        attention_kernel,
        grid_spec=grid_spec,
        out_shape=[
            jax.ShapeDtypeStruct(queries.shape, jnp.bfloat16),
            jax.ShapeDtypeStruct(queries.shape, jnp.bfloat16),
            jax.ShapeDtypeStruct(stock.shape[1:], jnp.float32),
            jax.ShapeDtypeStruct(stock.shape, jnp.bfloat16),
        ],
        compiler_params=pltpu.CompilerParams(dimension_semantics=("arbitrary",)),
        cost_estimate=pl.CostEstimate(
            flops=flops, transcendentals=blocks * rows * 3 * rows * (cols // HEAD_DIM),
            bytes_accessed=bytes_accessed,
        ),
    )(slot_ids, counts, queries, out_grad, stock)


def on_device(
    queries, encoder, key_weight, value_weight, out_grad, block_lists, list_counts, outer, inner
):
    blk = ("bz", "byx")
    position = lax.axis_index(blk)
    head_cols = key_weight.shape[1]
    model = encoder.shape[1]
    rows = encoder.shape[0]
    slice_rows = model // (outer * inner)
    pieces = encoder.reshape(rows, outer, inner, slice_rows).transpose(2, 0, 1, 3)
    picked = lax.all_to_all(
        pieces.reshape(inner, rows, outer * slice_rows), "byx", 0, 0, tiled=False
    ).reshape(inner * rows, outer * slice_rows)
    own_keys = jnp.dot(encoder, key_weight, preferred_element_type=jnp.float32).astype(jnp.bfloat16)
    own_values = jnp.dot(encoder, value_weight, preferred_element_type=jnp.float32).astype(
        jnp.bfloat16
    )
    own = jnp.stack([own_keys, own_values], 0)
    arrived = []
    for offset in range(-REACH, REACH + 1):
        if offset == 0:
            arrived.append(own)
        else:
            arrived.append(passed_along(own, blk, -offset, outer * inner))
    stock = jnp.stack(arrived, 0)
    slot_ids = (block_lists - (position - REACH)).astype(jnp.int32)
    attended, query_grad, owned, sending = attention(
        queries, out_grad, stock, slot_ids, list_counts.astype(jnp.int32)
    )
    for offset in range(-REACH, REACH + 1):
        if offset != 0:
            sent = sending[REACH + offset]
            owned = owned + passed_along(sent, blk, offset, outer * inner).astype(jnp.float32)
    rounded = owned.astype(jnp.bfloat16)
    contract_cols = (((1,), (1,)), ((), ()))
    encoder_terms = lax.dot_general(
        rounded[0], key_weight, contract_cols, preferred_element_type=jnp.float32
    ) + lax.dot_general(rounded[1], value_weight, contract_cols, preferred_element_type=jnp.float32)
    encoder_grad = lax.psum_scatter(encoder_terms, "grp", scatter_dimension=1, tiled=True).astype(
        jnp.bfloat16
    )
    both_grads = jnp.concatenate([rounded[0], rounded[1]], 1)
    group_grads = lax.all_gather(both_grads, "byx", axis=0, tiled=True)
    partial = lax.dot_general(
        picked, group_grads, (((0,), (0,)), ((), ())), preferred_element_type=jnp.float32
    )
    weight_rows = lax.psum_scatter(partial, "bz", scatter_dimension=0, tiled=True)
    return (
        attended,
        query_grad,
        encoder_grad,
        weight_rows[:, :head_cols],
        weight_rows[:, head_cols:],
    )


def solution(mesh):
    blk_size, grp_size = mesh.devices.shape
    outer = 4 if blk_size % 4 == 0 else 1
    inner = blk_size // outer
    split = jax.sharding.Mesh(
        mesh.devices.reshape(outer, inner, grp_size), ("bz", "byx", "grp")
    )
    blk = ("bz", "byx")
    in_specs = (
        P(blk, "grp"),
        P(blk, None),
        P(None, "grp"),
        P(None, "grp"),
        P(blk, "grp"),
        P(blk, None),
        P(blk),
    )
    out_specs = (
        P(blk, "grp"),
        P(blk, "grp"),
        P(blk, "grp"),
        P(blk, "grp"),
        P(blk, "grp"),
    )
    return jax.shard_map(
        functools.partial(on_device, outer=outer, inner=inner),
        mesh=split,
        in_specs=in_specs,
        out_specs=out_specs,
        check_vma=False,
    )
```

```python
import functools

import jax
import jax.numpy as jnp
from jax import lax
from jax.experimental import pallas as pl
from jax.experimental.pallas import tpu as pltpu
from jax.sharding import PartitionSpec as P

HEAD_DIM = 64
REACH = 4
LISTED = 5
LANES = 128


def passed_along(value, axis, by, size):
    pairs = [(i, i + by) for i in range(size) if 0 <= i + by < size]
    return lax.ppermute(value, axis, pairs)


def attention_kernel(
    slots_ref, counts_ref, q_ref, g_ref, stock_ref, out_ref, dq_ref, own_ref,
    sent_ref, acc_ref, flipped_ref,
):
    factor = HEAD_DIM ** (-0.5)
    step = pl.program_id(0)

    @pl.when(step == 0)
    def _():
        acc_ref[...] = jnp.zeros_like(acc_ref)

        def flip(s, carry):
            for kind in range(2):
                for p in range(stock_ref.shape[3] // LANES):
                    piece = stock_ref[s, kind, :, pl.ds(p * LANES, LANES)]
                    flipped_ref[s, kind, pl.ds(p * LANES, LANES), :] = (
                        piece.astype(jnp.float32).T.astype(flipped_ref.dtype)
                    )
            return carry

        lax.fori_loop(0, stock_ref.shape[0], flip, 0)

    count = counts_ref[step]
    rows = q_ref.shape[0]
    lane = lax.broadcasted_iota(jnp.int32, (rows, LANES), 1)
    first = lane < HEAD_DIM
    row = lax.broadcasted_iota(jnp.int32, (LANES, rows), 0)
    top = row < HEAD_DIM
    slots = [slots_ref[step, j] for j in range(LISTED)]
    f32 = jnp.float32
    bf16 = jnp.bfloat16

    def dot(a, b):
        return jnp.dot(a, b, preferred_element_type=f32)

    def run(used):
        def pair(p, carry):
            off = pl.multiple_of(p * LANES, LANES)
            qp = q_ref[:, pl.ds(off, LANES)]
            gp = g_ref[:, pl.ds(off, LANES)]
            qt = qp.astype(f32).T * factor
            gt = gp.astype(f32).T * factor
            zf = jnp.zeros_like(qt)
            qst = [jnp.where(top, qt, zf).astype(bf16), jnp.where(top, zf, qt).astype(bf16)]
            gst = [jnp.where(top, gt, zf).astype(bf16), jnp.where(top, zf, gt).astype(bf16)]
            zq = jnp.zeros_like(qp)
            qh = [jnp.where(first, qp, zq), jnp.where(first, zq, qp)]
            gh = [jnp.where(first, gp, zq), jnp.where(first, zq, gp)]
            ks = [stock_ref[slots[j], 0, :, pl.ds(off, LANES)] for j in range(used)]
            vs = [stock_ref[slots[j], 1, :, pl.ds(off, LANES)] for j in range(used)]
            kts = [flipped_ref[slots[j], 0, pl.ds(off, LANES), :] for j in range(used)]
            vts = [flipped_ref[slots[j], 1, pl.ds(off, LANES), :] for j in range(used)]
            outs, dqs = [], []
            dks = [None] * used
            dvs = [None] * used
            for h in range(2):
                scores = [dot(ks[j], qst[h]) for j in range(used)]
                peak = jnp.max(scores[0], axis=0, keepdims=True)
                for j in range(1, used):
                    peak = jnp.maximum(peak, jnp.max(scores[j], axis=0, keepdims=True))
                expos = [jnp.exp(sc - peak) for sc in scores]
                total = jnp.sum(expos[0], axis=0, keepdims=True)
                for j in range(1, used):
                    total = total + jnp.sum(expos[j], axis=0, keepdims=True)
                inverse = 1.0 / total
                ws = [(e * inverse).astype(bf16) for e in expos]
                out = dot(vts[0], ws[0])
                for j in range(1, used):
                    out = out + dot(vts[j], ws[j])
                dws = [dot(vs[j], gst[h]) for j in range(used)]
                wf = [w.astype(f32) for w in ws]
                center = jnp.sum(wf[0] * dws[0], axis=0, keepdims=True)
                for j in range(1, used):
                    center = center + jnp.sum(wf[j] * dws[j], axis=0, keepdims=True)
                dss = [(wf[j] * (dws[j] - center)).astype(bf16) for j in range(used)]
                dq = dot(kts[0], dss[0])
                for j in range(1, used):
                    dq = dq + dot(kts[j], dss[j])
                for j in range(used):
                    dk = dot(dss[j], qh[h])
                    dv = dot(ws[j], gh[h])
                    dks[j] = dk if dks[j] is None else dks[j] + dk
                    dvs[j] = dv if dvs[j] is None else dvs[j] + dv
                outs.append(out)
                dqs.append(dq)
            out_ref[:, pl.ds(off, LANES)] = jnp.where(top, outs[0], outs[1]).T.astype(out_ref.dtype)
            dq_ref[:, pl.ds(off, LANES)] = jnp.where(top, dqs[0], dqs[1]).T.astype(dq_ref.dtype)
            for j in range(used):
                acc_ref[slots[j], 0, :, pl.ds(off, LANES)] += dks[j]
                acc_ref[slots[j], 1, :, pl.ds(off, LANES)] += dvs[j]
            return carry

        lax.fori_loop(0, q_ref.shape[1] // LANES, pair, 0, unroll=True)

    for used in range(1, LISTED + 1):
        pl.when(count == used)(functools.partial(run, used))

    @pl.when(step == pl.num_programs(0) - 1)
    def _():
        own_ref[...] = acc_ref[REACH]
        sent_ref[...] = acc_ref[...].astype(sent_ref.dtype)


def attention(queries, out_grad, stock, slot_ids, counts):
    rows, cols = stock.shape[2], stock.shape[3]
    blocks = queries.shape[0] // rows
    n_slots = stock.shape[0]
    flops = blocks * (cols // LANES) * 2 * 3 * 6 * 2 * rows * LANES * LANES
    bytes_accessed = 4 * queries.size * 2 + stock.size * 2 + stock.size * 4
    grid_spec = pltpu.PrefetchScalarGridSpec(
        num_scalar_prefetch=2,
        grid=(blocks,),
        in_specs=[
            pl.BlockSpec((rows, cols), lambda i, s, c: (i, 0)),
            pl.BlockSpec((rows, cols), lambda i, s, c: (i, 0)),
            pl.BlockSpec((n_slots, 2, rows, cols), lambda i, s, c: (0, 0, 0, 0)),
        ],
        out_specs=[
            pl.BlockSpec((rows, cols), lambda i, s, c: (i, 0)),
            pl.BlockSpec((rows, cols), lambda i, s, c: (i, 0)),
            pl.BlockSpec((2, rows, cols), lambda i, s, c: (0, 0, 0)),
            pl.BlockSpec((n_slots, 2, rows, cols), lambda i, s, c: (0, 0, 0, 0)),
        ],
        scratch_shapes=[
            pltpu.VMEM(stock.shape, jnp.float32),
            pltpu.VMEM((n_slots, 2, cols, rows), stock.dtype),
        ],
    )
    return pl.pallas_call(
        attention_kernel,
        grid_spec=grid_spec,
        out_shape=[
            jax.ShapeDtypeStruct(queries.shape, jnp.bfloat16),
            jax.ShapeDtypeStruct(queries.shape, jnp.bfloat16),
            jax.ShapeDtypeStruct(stock.shape[1:], jnp.float32),
            jax.ShapeDtypeStruct(stock.shape, jnp.bfloat16),
        ],
        compiler_params=pltpu.CompilerParams(dimension_semantics=("arbitrary",)),
        cost_estimate=pl.CostEstimate(
            flops=flops, transcendentals=blocks * rows * 3 * rows * (cols // HEAD_DIM),
            bytes_accessed=bytes_accessed,
        ),
    )(slot_ids, counts, queries, out_grad, stock)


def on_device(
    queries, encoder, key_weight, value_weight, out_grad, block_lists, list_counts, outer, inner
):
    blk = ("bz", "byx")
    position = lax.axis_index(blk)
    head_cols = key_weight.shape[1]
    model = encoder.shape[1]
    own_keys = jnp.dot(encoder, key_weight, preferred_element_type=jnp.float32).astype(jnp.bfloat16)
    own_values = jnp.dot(encoder, value_weight, preferred_element_type=jnp.float32).astype(
        jnp.bfloat16
    )
    own = jnp.stack([own_keys, own_values], 0)
    arrived = []
    for offset in range(-REACH, REACH + 1):
        if offset == 0:
            arrived.append(own)
        else:
            arrived.append(passed_along(own, blk, -offset, outer * inner))
    stock = jnp.stack(arrived, 0)
    late_encoder, stock = lax.optimization_barrier((encoder, stock))
    near = lax.all_gather(late_encoder, "byx", axis=0, tiled=False)
    slot_ids = (block_lists - (position - REACH)).astype(jnp.int32)
    attended, query_grad, owned, sending = attention(
        queries, out_grad, stock, slot_ids, list_counts.astype(jnp.int32)
    )
    for offset in range(-REACH, REACH + 1):
        if offset != 0:
            sent = sending[REACH + offset]
            owned = owned + passed_along(sent, blk, offset, outer * inner).astype(jnp.float32)
    rounded = owned.astype(jnp.bfloat16)
    contract_cols = (((1,), (1,)), ((), ()))
    encoder_terms = lax.dot_general(
        rounded[0], key_weight, contract_cols, preferred_element_type=jnp.float32
    ) + lax.dot_general(rounded[1], value_weight, contract_cols, preferred_element_type=jnp.float32)
    encoder_grad = lax.psum_scatter(encoder_terms, "grp", scatter_dimension=1, tiled=True).astype(
        jnp.bfloat16
    )
    both_grads = jnp.concatenate([rounded[0], rounded[1]], 1)
    group_grads = lax.all_gather(both_grads, "byx", axis=0, tiled=True)
    rows = encoder.shape[0]
    slice_rows = model // (outer * inner)
    picked = lax.dynamic_slice_in_dim(
        near.reshape(inner * rows, outer, inner, slice_rows),
        lax.axis_index("byx"),
        1,
        axis=2,
    ).reshape(inner * rows, outer * slice_rows)
    partial = lax.dot_general(
        picked, group_grads, (((0,), (0,)), ((), ())), preferred_element_type=jnp.float32
    )
    weight_rows = lax.psum_scatter(partial, "bz", scatter_dimension=0, tiled=True)
    return (
        attended,
        query_grad,
        encoder_grad,
        weight_rows[:, :head_cols],
        weight_rows[:, head_cols:],
    )


def solution(mesh):
    blk_size, grp_size = mesh.devices.shape
    outer = 4 if blk_size % 4 == 0 else 1
    inner = blk_size // outer
    split = jax.sharding.Mesh(
        mesh.devices.reshape(outer, inner, grp_size), ("bz", "byx", "grp")
    )
    blk = ("bz", "byx")
    in_specs = (
        P(blk, "grp"),
        P(blk, None),
        P(None, "grp"),
        P(None, "grp"),
        P(blk, "grp"),
        P(blk, None),
        P(blk),
    )
    out_specs = (
        P(blk, "grp"),
        P(blk, "grp"),
        P(blk, "grp"),
        P(blk, "grp"),
        P(blk, "grp"),
    )
    return jax.shard_map(
        functools.partial(on_device, outer=outer, inner=inner),
        mesh=split,
        in_specs=in_specs,
        out_specs=out_specs,
        check_vma=False,
    )
```
